256 devices in a mesh: ctx: 64 (over z, y, core), head: 4 (over x).
Axes of the slice: x: 4, y: 4, z: 8, core: 2. Of those that a mesh axis runs over, the one named last changes fastest.
Arguments:
- delta_q: bfloat16 [16384, 2048], P('ctx', 'head'), may hold values from -6 to 6
- delta_k: bfloat16 [16384, 2048], P('ctx', 'head'), may hold values from -6 to 6
- delta_v: bfloat16 [16384, 2048], P('ctx', 'head'), may hold values from -6 to 6
- beta: float32 [16384, 16], P('ctx', 'head'), may hold values from 0 to 0.9, as said below
- log_decay: float32 [16384, 16], P('ctx', 'head'), may hold values from -1 to 0, as said below
- out_gate: bfloat16 [16384, 2048], P('ctx', 'head'), may hold values from -6 to 6
- norm_gain: float32 [128], replicated, may hold values from 0.1 to 1.9
- attn_q: bfloat16 [16384, 2048], P('ctx', 'head'), may hold values from -16 to 16
- attn_k: bfloat16 [16384, 2048], P('ctx', 'head'), may hold values from -16 to 16
- attn_v: bfloat16 [16384, 2048], P('ctx', 'head'), may hold values from -6 to 6
- w_delta_out: bfloat16 [2048, 2048], P('head'), may hold values from -0.125 to 0.125
- w_attn_out: bfloat16 [2048, 2048], P('head'), may hold values from -0.125 to 0.125
Outputs:
- branch_sum: bfloat16 [16384, 2048], P(('ctx', 'head'))
The draws below stay inside these ranges and needn't reach their ends.
Inputs may be any that keep to these rules, and one draw needn't show every extreme that they name: `beta`: write strengths, positive. `log_decay`: log decays, negative.
All inputs are finite; a program needn't handle non-finite values.
Results may differ from the reference program's by a relative error of at most 0.022.
Values may be sent and summed in bfloat16 or wider, within the bound.
No kernel may reach another device: no remote copies, remote signals or barrier semaphores. Data moves between devices by JAX's collectives and lax.ppermute only.
A program may use at most 128 MiB of HBM per device.

```python
import math
import jax
import jax.numpy as jnp
from jax import lax

D = 2048
H = 16
DH = 128
WINDOW = 1024
TOKENS_PER_PART = 256
SEQUENCE_TOKENS = 16384
N_HEAD = 4


def speeds_of_heads(key):
    return jax.random.uniform(jax.random.fold_in(key, 11), (H,), jnp.float32)


def draw_beta(key, part):
    head_speed = speeds_of_heads(key)
    fast_log = math.log(0.6)
    slow_log = math.log(0.5 * DH / SEQUENCE_TOKENS)
    base_rate = jnp.exp(fast_log * (1.0 - head_speed) + slow_log * head_speed)
    roughness = jax.random.uniform(jax.random.fold_in(key, 16), (SEQUENCE_TOKENS, H), jnp.float32, 0.5, 1.5)
    return jnp.minimum(base_rate[None, :] * roughness, 0.9)


def draw_log_decay(key, part):
    head_speed = speeds_of_heads(key)
    fast_log = math.log(1.0 / 40.0)
    slow_log = math.log(0.5 / SEQUENCE_TOKENS)
    base_rate = jnp.exp(fast_log * (1.0 - head_speed) + slow_log * head_speed)
    device_scale = jnp.exp(jax.random.uniform(jax.random.fold_in(key, 12), (SEQUENCE_TOKENS // TOKENS_PER_PART, H), jnp.float32, -math.log(2.0), math.log(2.0)))
    device_scale = jnp.repeat(device_scale, TOKENS_PER_PART, axis=0)
    roughness = jax.random.uniform(jax.random.fold_in(key, 13), (SEQUENCE_TOKENS, H), jnp.float32, 0.5, 1.5)
    steady = -base_rate[None, :] * device_scale * roughness
    transfer_groups = jax.random.randint(jax.random.fold_in(key, 14), (3,), 0, SEQUENCE_TOKENS)
    masked_entries = jnp.any(jnp.arange(SEQUENCE_TOKENS)[:, None] == transfer_groups[None, :], axis=1)
    sudden = jnp.log(jax.random.uniform(jax.random.fold_in(key, 15), (SEQUENCE_TOKENS, H), jnp.float32, 0.5, 0.8))
    return jnp.where(masked_entries[:, None], sudden, steady)


def draw_attn_q(key, part):
    shape = (SEQUENCE_TOKENS, H * DH)
    return jnp.clip(jax.random.normal(jax.random.fold_in(key, 21), shape, jnp.float32), -4.0, 4.0).astype(jnp.bfloat16)


def draw_attn_k(key, part):
    shape = (SEQUENCE_TOKENS, H * DH)
    return jnp.clip(jax.random.normal(jax.random.fold_in(key, 22), shape, jnp.float32), -4.0, 4.0).astype(jnp.bfloat16)


def steps_of(key, dims, cuts, smallest, top_value):
    def one(dim, blocks):
        heights = jax.random.uniform(jax.random.fold_in(jax.random.fold_in(key, 6), dim), (blocks,), jnp.float32, smallest / len(cuts), top_value / len(cuts))
        return jnp.repeat(jnp.exp(heights), dims[dim] // blocks).reshape((-1,) + (1,) * (len(dims) - dim - 1))

    level = one(*cuts[0])
    for cut in cuts[1:]:
        level = level * one(*cut)
    return level


def centred(stream_key, extent, deviation, most, shards=(), kind=jnp.bfloat16):
    values = jax.random.normal(stream_key, extent, jnp.float32) * deviation
    if len(shards) > 0:
        values = steps_of(stream_key, extent, shards, -0.22, 0.18) * values
    return jnp.clip(values, min=-most, max=most).astype(kind)


def setup_inputs(seed: int = 0) -> dict:
    keys = jax.random.split(jax.random.key(seed), 13)
    delta_q = centred(keys[0], (SEQUENCE_TOKENS, H * DH), 1.0, 6.0, ((0, 64), (1, 4)))
    delta_k = centred(keys[1], (SEQUENCE_TOKENS, H * DH), 1.0, 6.0, ((0, 64), (1, 4)))
    delta_v = centred(keys[2], (SEQUENCE_TOKENS, H * DH), 1.0, 6.0, ((0, 64), (1, 4)))
    beta = draw_beta(jax.random.fold_in(keys[12], 71), 0)
    log_decay = draw_log_decay(jax.random.fold_in(keys[12], 71), 0)
    out_gate = centred(keys[5], (SEQUENCE_TOKENS, H * DH), 1.0, 6.0, ((0, 64), (1, 4)))
    norm_gain = jnp.clip(1.0 + 0.18 * jax.random.normal(keys[6], (DH,), jnp.float32), 0.1, 1.9)
    attn_q = draw_attn_q(jax.random.fold_in(keys[12], 71), 0)
    attn_k = draw_attn_k(jax.random.fold_in(keys[12], 71), 0)
    attn_v = centred(keys[9], (SEQUENCE_TOKENS, H * DH), 1.0, 6.0, ((0, 64), (1, 4)))
    w_delta_out = centred(keys[10], (H * DH, D), (H * DH) ** -0.5, 0.125, ((0, 4),))
    w_attn_out = centred(keys[11], (H * DH, D), (H * DH) ** -0.5, 0.125, ((0, 4),))
    return {"delta_q": delta_q, "delta_k": delta_k, "delta_v": delta_v, "beta": beta, "log_decay": log_decay, "out_gate": out_gate, "norm_gain": norm_gain, "attn_q": attn_q, "attn_k": attn_k, "attn_v": attn_v, "w_delta_out": w_delta_out, "w_attn_out": w_attn_out}


highest = lax.Precision.HIGHEST

def unit_rows(array):
    return array / jnp.sqrt(lax.optimization_barrier(jnp.sum(array * array, axis=-1, keepdims=True)) + 1e-06)

def unit_inverse(lower_part):
    order_len = lower_part.shape[-1]
    identity = jnp.eye(order_len, dtype=jnp.float32)
    powered = -lower_part
    result = identity + powered
    for counter in range(1, max(1, (order_len - 1).bit_length())):
        powered = jnp.matmul(powered, powered, precision=highest)
        result = jnp.matmul(result, identity + powered, precision=highest)
    return result

def block_terms(queries, keys_in, values_in, betas, log_rates):
    cumulative = jnp.cumsum(log_rates, axis=-1)
    length = queries.shape[-2]
    positions = jnp.arange(length)
    strict = positions[:, None] > positions[None, :]
    inclusive = positions[:, None] >= positions[None, :]
    spread = cumulative[..., :, None] - cumulative[..., None, :]
    ratio_strict = jnp.where(strict, jnp.exp(jnp.where(strict, spread, 0.0)), 0.0)
    ratio_incl = jnp.where(inclusive, jnp.exp(jnp.where(inclusive, spread, 0.0)), 0.0)
    key_gram = jnp.einsum('...td,...sd->...ts', keys_in, keys_in, precision=highest)
    inverse = unit_inverse(betas[..., :, None] * ratio_strict * key_gram)
    decayed = jnp.exp(cumulative)
    pseudo = jnp.matmul(inverse, betas[..., None] * values_in, precision=highest)
    writer = jnp.matmul(inverse, (betas * decayed)[..., None] * keys_in, precision=highest)
    to_end = jnp.exp(cumulative[..., -1:] - cumulative)
    keys_end = keys_in * to_end[..., None]
    identity = jnp.eye(queries.shape[-1], dtype=jnp.float32)
    transition = jnp.exp(cumulative[..., -1])[..., None, None] * identity - jnp.einsum('...td,...te->...de', keys_end, writer, precision=highest)
    contrib = jnp.einsum('...td,...te->...de', keys_end, pseudo, precision=highest)
    mixing = ratio_incl * jnp.einsum('...td,...sd->...ts', queries, keys_in, precision=highest)
    local_out = jnp.matmul(mixing, pseudo, precision=highest)
    carry_out = decayed[..., None] * queries - jnp.matmul(mixing, writer, precision=highest)
    return (transition, contrib, local_out, carry_out)

def window_block(queries, keys_in, values_in, query_pos, key_pos):
    scores = jnp.einsum('thd,shd->hts', queries.astype(jnp.float32), keys_in.astype(jnp.float32)) * DH ** (-0.5)
    offsets = query_pos[:, None] - key_pos[None, :]
    inside = (offsets >= 0) & (offsets < WINDOW) & (key_pos[None, :] >= 0)
    masked = jnp.where(inside[None], scores, -1e+30)
    block_max = lax.optimization_barrier(jnp.max(masked, axis=-1))
    weights = jnp.where(inside[None], jnp.exp(masked - block_max[..., None]), 0.0)
    probs = weights.astype(jnp.bfloat16)
    block_num = jnp.einsum('hts,shd->htd', probs.astype(jnp.float32), values_in.astype(jnp.float32))
    block_den = lax.optimization_barrier(jnp.sum(weights, axis=-1))
    return (block_max, block_num, block_den)

def group_sum(delta_heads, w_delta, attn_heads, w_attn):
    columns = H * DH // N_HEAD
    total = jnp.zeros((delta_heads.shape[0], w_delta.shape[1]), jnp.float32)
    for group in range(N_HEAD):
        low = group * columns
        high = (group + 1) * columns
        partial_term = jnp.dot(delta_heads[:, low:high], w_delta[low:high], preferred_element_type=jnp.float32)
        partial_term = partial_term + jnp.dot(attn_heads[:, low:high], w_attn[low:high], preferred_element_type=jnp.float32)
        rounded = partial_term.astype(jnp.bfloat16)
        total = total + lax.optimization_barrier(rounded).astype(jnp.float32)
    return total

def reference(delta_q, delta_k, delta_v, beta, log_decay, out_gate, norm_gain, attn_q, attn_k, attn_v, w_delta_out, w_attn_out):
    block_len = min(64, SEQUENCE_TOKENS)
    blocks = SEQUENCE_TOKENS // block_len

    def heads_blocks(array):
        return array.astype(jnp.float32).reshape(blocks, block_len, H, DH).transpose(0, 2, 1, 3)
    queries = unit_rows(heads_blocks(delta_q)) * DH ** (-0.5)
    keys_in = unit_rows(heads_blocks(delta_k))
    values_in = heads_blocks(delta_v)
    betas = beta.reshape(blocks, block_len, H).transpose(0, 2, 1)
    log_rates = log_decay.reshape(blocks, block_len, H).transpose(0, 2, 1)

    def advance(state, inputs):
        transition, contrib, local_out, carry_out = block_terms(*inputs)
        outputs = local_out + jnp.matmul(carry_out, state, precision=highest)
        return (jnp.matmul(transition, state, precision=highest) + contrib, outputs)
    initial = jnp.zeros((H, DH, DH), jnp.float32)
    final_state, delta_raw = lax.scan(advance, initial, (queries, keys_in, values_in, betas, log_rates))
    delta_raw = delta_raw.transpose(0, 2, 1, 3).reshape(SEQUENCE_TOKENS, H, DH)
    gate_act = jax.nn.silu(out_gate.astype(jnp.float32).reshape(SEQUENCE_TOKENS, H, DH))
    normed = delta_raw / jnp.sqrt(lax.optimization_barrier(jnp.mean(delta_raw * delta_raw, axis=-1, keepdims=True)) + 1e-06) * norm_gain * gate_act
    delta_heads = normed.reshape(SEQUENCE_TOKENS, H * DH).astype(jnp.bfloat16)
    span = WINDOW // TOKENS_PER_PART

    def attend(block_index):
        query_start = (block_index * TOKENS_PER_PART).astype(jnp.int32)
        query_rows = lax.dynamic_slice_in_dim(attn_q, query_start, TOKENS_PER_PART, 0).reshape(TOKENS_PER_PART, H, DH)
        query_pos = query_start + jnp.arange(TOKENS_PER_PART, dtype=jnp.int32)
        maxima, numers, denoms = ([], [], [])
        for back in range(span + 1):
            source = block_index - back
            key_start = (jnp.maximum(source, 0) * TOKENS_PER_PART).astype(jnp.int32)
            key_rows = lax.dynamic_slice_in_dim(attn_k, key_start, TOKENS_PER_PART, 0).reshape(TOKENS_PER_PART, H, DH)
            value_rows = lax.dynamic_slice_in_dim(attn_v, key_start, TOKENS_PER_PART, 0).reshape(TOKENS_PER_PART, H, DH)
            key_pos = (source * TOKENS_PER_PART).astype(jnp.int32) + jnp.arange(TOKENS_PER_PART, dtype=jnp.int32)
            block_max, block_num, block_den = window_block(query_rows, key_rows, value_rows, query_pos, key_pos)
            maxima.append(block_max)
            numers.append(block_num)
            denoms.append(block_den)
        top = maxima[0]
        for block_max in maxima[1:]:
            top = jnp.maximum(top, block_max)
        numer = jnp.zeros_like(numers[0])
        denom = jnp.zeros_like(denoms[0])
        for block_max, block_num, block_den in zip(maxima, numers, denoms):
            factor = jnp.exp(block_max - top)
            numer = numer + factor[..., None] * block_num
            denom = denom + factor * block_den
        result = numer / denom[..., None]
        return result.transpose(1, 0, 2).reshape(TOKENS_PER_PART, H * DH).astype(jnp.bfloat16)
    attn_heads = lax.map(attend, jnp.arange(SEQUENCE_TOKENS // TOKENS_PER_PART, dtype=jnp.int32)).reshape(SEQUENCE_TOKENS, H * DH)
    total = group_sum(delta_heads, w_delta_out, attn_heads, w_attn_out)
    return total.astype(jnp.bfloat16)
```

```python
import jax
import jax.numpy as jnp
from jax import lax
from jax.sharding import PartitionSpec as P

DH = 128
WINDOW = 1024


highest = lax.Precision.HIGHEST


def prefix_state(pair, axis):
    place = lax.axis_index(axis)
    size = lax.axis_size(axis)
    mat, vec = pair
    distance = 1
    while distance < size:
        if 2 * distance >= size:
            far_vec = passed_along(vec.astype(jnp.bfloat16), axis, distance).astype(jnp.float32)
            vec = jnp.einsum("hij,hjk->hik", mat, far_vec, precision=highest) + vec
        else:
            far_mat, far_vec = passed_along(
                (mat.astype(jnp.bfloat16), vec.astype(jnp.bfloat16)), axis, distance
            )
            joined = chain_pairs((far_mat.astype(jnp.float32), far_vec.astype(jnp.float32)), (mat, vec))
            mat = jnp.where(place >= distance, joined[0], mat)
            vec = jnp.where(place >= distance, joined[1], vec)
        distance *= 2
    return passed_along(vec.astype(jnp.bfloat16), axis, 1).astype(jnp.float32)


def passed_along(block, axis, distance):
    devices = range(lax.axis_size(axis))
    route = [(i - distance, i) for i in devices if i - distance in devices]
    return lax.ppermute(block, axis, route)


def unit_rows(array):
    return array / jnp.sqrt(jnp.sum(array * array, axis=-1, keepdims=True) + 1e-06)


def unit_inverse(lower_part):
    order_len = lower_part.shape[-1]
    identity = jnp.eye(order_len, dtype=jnp.float32)
    powered = -lower_part
    result = identity + powered
    for counter in range(1, max(1, (order_len - 1).bit_length())):
        powered = jnp.matmul(powered, powered, precision=highest)
        result = jnp.matmul(result, identity + powered, precision=highest)
    return result


def block_terms(queries, keys_in, values_in, betas, log_rates):
    cumulative = jnp.cumsum(log_rates, axis=-1)
    length = queries.shape[-2]
    positions = jnp.arange(length)
    strict = positions[:, None] > positions[None, :]
    inclusive = positions[:, None] >= positions[None, :]
    spread = cumulative[..., :, None] - cumulative[..., None, :]
    ratio_strict = jnp.where(strict, jnp.exp(jnp.where(strict, spread, 0.0)), 0.0)
    ratio_incl = jnp.where(inclusive, jnp.exp(jnp.where(inclusive, spread, 0.0)), 0.0)
    key_gram = jnp.einsum("...td,...sd->...ts", keys_in, keys_in, precision=highest)
    inverse = unit_inverse(betas[..., :, None] * ratio_strict * key_gram)
    decayed = jnp.exp(cumulative)
    pseudo = jnp.matmul(inverse, betas[..., None] * values_in, precision=highest)
    writer = jnp.matmul(inverse, (betas * decayed)[..., None] * keys_in, precision=highest)
    to_end = jnp.exp(cumulative[..., -1:] - cumulative)
    keys_end = keys_in * to_end[..., None]
    identity = jnp.eye(queries.shape[-1], dtype=jnp.float32)
    transition = jnp.exp(cumulative[..., -1])[..., None, None] * identity - jnp.einsum(
        "...td,...te->...de", keys_end, writer, precision=highest
    )
    contrib = jnp.einsum("...td,...te->...de", keys_end, pseudo, precision=highest)
    mixing = ratio_incl * jnp.einsum("...td,...sd->...ts", queries, keys_in, precision=highest)
    local_out = jnp.matmul(mixing, pseudo, precision=highest)
    carry_out = decayed[..., None] * queries - jnp.matmul(mixing, writer, precision=highest)
    return (transition, contrib, local_out, carry_out)


def window_block(queries, keys_in, values_in, query_pos, key_pos):
    scores = jnp.einsum(
        "thd,shd->hts", queries, keys_in, preferred_element_type=jnp.float32
    ) * DH ** (-0.5)
    offsets = query_pos[:, None] - key_pos[None, :]
    inside = (offsets >= 0) & (offsets < WINDOW) & (key_pos[None, :] >= 0)
    masked = jnp.where(inside[None], scores, -1e30)
    block_max = jnp.max(masked, axis=-1)
    weights = jnp.where(inside[None], jnp.exp(masked - block_max[..., None]), 0.0)
    probs = weights.astype(jnp.bfloat16)
    block_num = jnp.einsum("hts,shd->htd", probs, values_in, preferred_element_type=jnp.float32)
    block_den = jnp.sum(weights, axis=-1)
    return (block_max, block_num, block_den)


def chain_pairs(earlier, later):
    matrix = jnp.einsum("hij,hjk->hik", later[0], earlier[0], precision=highest)
    vector = jnp.einsum("hij,hjk->hik", later[0], earlier[1], precision=highest) + later[1]
    return (matrix, vector)


def shards(
    delta_q,
    delta_k,
    delta_v,
    beta,
    log_decay,
    out_gate,
    norm_gain,
    attn_q,
    attn_k,
    attn_v,
    w_delta_out,
    w_attn_out,
):
    rows_here = delta_q.shape[0]
    local_heads = delta_q.shape[1] // DH
    block_len = min(64, rows_here)
    blocks = rows_here // block_len

    def heads_blocks(array):
        return (
            array.astype(jnp.float32)
            .reshape(blocks, block_len, local_heads, DH)
            .transpose(2, 0, 1, 3)
        )

    queries = unit_rows(heads_blocks(delta_q)) * DH ** (-0.5)
    keys_in = unit_rows(heads_blocks(delta_k))
    values_in = heads_blocks(delta_v)
    betas = beta.reshape(blocks, block_len, local_heads).transpose(2, 0, 1)
    log_rates = log_decay.reshape(blocks, block_len, local_heads).transpose(2, 0, 1)
    transition, contrib, local_out, carry_out = block_terms(
        queries, keys_in, values_in, betas, log_rates
    )
    identity = jnp.broadcast_to(jnp.eye(DH, dtype=jnp.float32), (local_heads, DH, DH))
    zero_state = jnp.zeros((local_heads, DH, DH), jnp.float32)

    def compose(carried, inputs):
        after_pair = chain_pairs(carried, inputs)
        return (after_pair, carried)

    shard_pair, starts = lax.scan(
        compose,
        (identity, zero_state),
        (transition.transpose(1, 0, 2, 3), contrib.transpose(1, 0, 2, 3)),
    )
    start_mats = starts[0].transpose(1, 0, 2, 3)
    start_vecs = starts[1].transpose(1, 0, 2, 3)
    own_out = local_out + jnp.einsum("hntd,hnde->hnte", carry_out, start_vecs, precision=highest)
    reach = jnp.einsum("hntd,hnde->hnte", carry_out, start_mats, precision=highest)
    incoming_state = prefix_state(shard_pair, "ctx")
    delta_raw = own_out + jnp.einsum("hntd,hde->hnte", reach, incoming_state, precision=highest)
    delta_raw = delta_raw.transpose(1, 2, 0, 3).reshape(rows_here, local_heads, DH)
    gate_act = jax.nn.silu(out_gate.astype(jnp.float32).reshape(rows_here, local_heads, DH))
    normed = (
        delta_raw
        / jnp.sqrt(jnp.mean(delta_raw * delta_raw, axis=-1, keepdims=True) + 1e-06)
        * norm_gain
        * gate_act
    )
    delta_heads = normed.reshape(rows_here, local_heads * DH).astype(jnp.bfloat16)
    position = lax.axis_index("ctx")
    query_rows = attn_q.reshape(rows_here, local_heads, DH)
    query_pos = position * rows_here + jnp.arange(rows_here, dtype=jnp.int32)
    maxima, numers, denoms = ([], [], [])
    own_max, own_num, own_den = window_block(
        query_rows,
        attn_k.reshape(rows_here, local_heads, DH),
        attn_v.reshape(rows_here, local_heads, DH),
        query_pos,
        query_pos,
    )
    maxima.append(own_max)
    numers.append(own_num)
    denoms.append(own_den)
    for back in range(1, WINDOW // rows_here + 1):
        keys_far, values_far = passed_along((attn_k, attn_v), "ctx", back)
        key_pos = (position - back) * rows_here + jnp.arange(rows_here, dtype=jnp.int32)
        remote_maximum, far_num, far_den = window_block(
            query_rows,
            keys_far.reshape(rows_here, local_heads, DH),
            values_far.reshape(rows_here, local_heads, DH),
            query_pos,
            key_pos,
        )
        maxima.append(remote_maximum)
        numers.append(far_num)
        denoms.append(far_den)
    top = maxima[0]
    for block_max in maxima[1:]:
        top = jnp.maximum(top, block_max)
    numer = jnp.zeros_like(numers[0])
    denom = jnp.zeros_like(denoms[0])
    for block_max, block_num, block_den in zip(maxima, numers, denoms):
        factor = jnp.exp(block_max - top)
        numer = numer + factor[..., None] * block_num
        denom = denom + factor * block_den
    attn_heads = (
        (numer / denom[..., None])
        .transpose(1, 0, 2)
        .reshape(rows_here, local_heads * DH)
        .astype(jnp.bfloat16)
    )
    running_partial_sum = jnp.dot(delta_heads, w_delta_out, preferred_element_type=jnp.float32)
    running_partial_sum = running_partial_sum + jnp.dot(
        attn_heads, w_attn_out, preferred_element_type=jnp.float32
    )
    n_head = lax.axis_size("head")
    pieces = lax.all_to_all(
        running_partial_sum.astype(jnp.bfloat16), "head", 0, 0, tiled=True
    )
    pieces = pieces.reshape(n_head, rows_here // n_head, pieces.shape[-1]).astype(jnp.float32)
    return jnp.sum(pieces, axis=0).astype(jnp.bfloat16)


def solution(mesh):
    return jax.shard_map(
        shards,
        mesh=mesh,
        in_specs=(
            P("ctx", "head"),
            P("ctx", "head"),
            P("ctx", "head"),
            P("ctx", "head"),
            P("ctx", "head"),
            P("ctx", "head"),
            P(),
            P("ctx", "head"),
            P("ctx", "head"),
            P("ctx", "head"),
            P("head", None),
            P("head", None),
        ),
        out_specs=P(("ctx", "head"), None),
        check_vma=False,
    )
```

```python
import jax
import jax.numpy as jnp
from jax import lax
from jax.sharding import PartitionSpec as P

DH = 128
WINDOW = 1024


highest = lax.Precision.HIGHEST


def prefix_state(pair, axis, fillers):
    place = lax.axis_index(axis)
    size = lax.axis_size(axis)
    mat, vec = pair
    width = mat.shape[-1]
    distance = 1
    done = []
    pending = list(fillers)

    def fill(far):
        if not pending:
            return far
        work, inputs = pending.pop(0)
        inputs, _ = lax.optimization_barrier((inputs, vec))
        result, far = lax.optimization_barrier((work(*inputs), far))
        done.append(result)
        return far

    while distance < size:
        if 2 * distance >= size:
            far_vec = passed_along(vec.astype(jnp.bfloat16), axis, distance)
            far_vec = fill(far_vec).astype(jnp.float32)
            vec = jnp.einsum("hij,hjk->hik", mat, far_vec, precision=highest) + vec
        else:
            packed = jnp.concatenate([mat, vec], axis=-1).astype(jnp.bfloat16)
            far = fill(passed_along(packed, axis, distance)).astype(jnp.float32)
            joined = jnp.einsum("hij,hjk->hik", mat, far, precision=highest)
            mat = jnp.where(place >= distance, joined[..., :width], mat)
            vec = joined[..., width:] + vec
        distance *= 2
    incoming = fill(passed_along(vec.astype(jnp.bfloat16), axis, 1)).astype(jnp.float32)
    while pending:
        work, inputs = pending.pop(0)
        done.append(work(*inputs))
    return incoming, done


def passed_along(block, axis, distance):
    devices = range(lax.axis_size(axis))
    route = [(i - distance, i) for i in devices if i - distance in devices]
    return lax.ppermute(block, axis, route)


def unit_rows(array):
    return array / jnp.sqrt(jnp.sum(array * array, axis=-1, keepdims=True) + 1e-06)


def unit_inverse(lower_part):
    order_len = lower_part.shape[-1]
    identity = jnp.eye(order_len, dtype=jnp.float32)
    powered = -lower_part
    result = identity + powered
    for counter in range(1, max(1, (order_len - 1).bit_length())):
        powered = jnp.matmul(powered, powered, precision=highest)
        result = jnp.matmul(result, identity + powered, precision=highest)
    return result


def block_terms(queries, keys_in, values_in, betas, log_rates):
    cumulative = jnp.cumsum(log_rates, axis=-1)
    length = queries.shape[-2]
    positions = jnp.arange(length)
    strict = positions[:, None] > positions[None, :]
    inclusive = positions[:, None] >= positions[None, :]
    spread = cumulative[..., :, None] - cumulative[..., None, :]
    ratio_strict = jnp.where(strict, jnp.exp(jnp.where(strict, spread, 0.0)), 0.0)
    ratio_incl = jnp.where(inclusive, jnp.exp(jnp.where(inclusive, spread, 0.0)), 0.0)
    key_gram = jnp.einsum("...td,...sd->...ts", keys_in, keys_in, precision=highest)
    inverse = unit_inverse(betas[..., :, None] * ratio_strict * key_gram)
    decayed = jnp.exp(cumulative)
    pseudo = jnp.matmul(inverse, betas[..., None] * values_in, precision=highest)
    writer = jnp.matmul(inverse, (betas * decayed)[..., None] * keys_in, precision=highest)
    to_end = jnp.exp(cumulative[..., -1:] - cumulative)
    keys_end = keys_in * to_end[..., None]
    identity = jnp.eye(queries.shape[-1], dtype=jnp.float32)
    transition = jnp.exp(cumulative[..., -1])[..., None, None] * identity - jnp.einsum(
        "...td,...te->...de", keys_end, writer, precision=highest
    )
    contrib = jnp.einsum("...td,...te->...de", keys_end, pseudo, precision=highest)
    return (transition, contrib, (queries, keys_in, ratio_incl, decayed, pseudo, writer))


def block_outputs(queries, keys_in, ratio_incl, decayed, pseudo, writer):
    mixing = ratio_incl * jnp.einsum("...td,...sd->...ts", queries, keys_in, precision=highest)
    local_out = jnp.matmul(mixing, pseudo, precision=highest)
    carry_out = decayed[..., None] * queries - jnp.matmul(mixing, writer, precision=highest)
    return (local_out, carry_out)


def window_block(queries, keys_in, values_in, query_pos, key_pos):
    scores = jnp.einsum(
        "thd,shd->hts", queries, keys_in, preferred_element_type=jnp.float32
    ) * DH ** (-0.5)
    offsets = query_pos[:, None] - key_pos[None, :]
    inside = (offsets >= 0) & (offsets < WINDOW) & (key_pos[None, :] >= 0)
    masked = jnp.where(inside[None], scores, -1e30)
    block_max = jnp.max(masked, axis=-1)
    weights = jnp.where(inside[None], jnp.exp(masked - block_max[..., None]), 0.0)
    probs = weights.astype(jnp.bfloat16)
    block_num = jnp.einsum("hts,shd->htd", probs, values_in, preferred_element_type=jnp.float32)
    block_den = jnp.sum(weights, axis=-1)
    return (block_max, block_num, block_den)


def chain_pairs(earlier, later):
    matrix = jnp.einsum("hij,hjk->hik", later[0], earlier[0], precision=highest)
    vector = jnp.einsum("hij,hjk->hik", later[0], earlier[1], precision=highest) + later[1]
    return (matrix, vector)


def shards(
    delta_q,
    delta_k,
    delta_v,
    beta,
    log_decay,
    out_gate,
    norm_gain,
    attn_q,
    attn_k,
    attn_v,
    w_delta_out,
    w_attn_out,
):
    rows_here = delta_q.shape[0]
    local_heads = delta_q.shape[1] // DH
    block_len = min(64, rows_here)
    blocks = rows_here // block_len

    def heads_blocks(array):
        return (
            array.astype(jnp.float32)
            .reshape(blocks, block_len, local_heads, DH)
            .transpose(2, 0, 1, 3)
        )

    queries = unit_rows(heads_blocks(delta_q)) * DH ** (-0.5)
    keys_in = unit_rows(heads_blocks(delta_k))
    values_in = heads_blocks(delta_v)
    betas = beta.reshape(blocks, block_len, local_heads).transpose(2, 0, 1)
    log_rates = log_decay.reshape(blocks, block_len, local_heads).transpose(2, 0, 1)
    transition, contrib, out_terms = block_terms(queries, keys_in, values_in, betas, log_rates)
    identity = jnp.broadcast_to(jnp.eye(DH, dtype=jnp.float32), (local_heads, DH, DH))
    zero_state = jnp.zeros((local_heads, DH, DH), jnp.float32)
    start_mats = [identity]
    start_vecs = [zero_state]
    run_mat, run_vec = transition[:, 0], contrib[:, 0]
    for block in range(1, blocks):
        start_mats.append(run_mat)
        start_vecs.append(run_vec)
        joined = jnp.einsum(
            "hij,hjk->hik",
            transition[:, block],
            jnp.concatenate([run_mat, run_vec], axis=-1),
            precision=highest,
        )
        run_mat = joined[..., :DH]
        run_vec = joined[..., DH:] + contrib[:, block]
    start_mats = jnp.stack(start_mats, axis=1)
    start_vecs = jnp.stack(start_vecs, axis=1)
    shard_pair = (run_mat, run_vec)
    position = lax.axis_index("ctx")
    spans = WINDOW // rows_here
    far_blocks = [
        passed_along(jnp.concatenate([attn_k, attn_v], axis=-1), "ctx", back)
        for back in range(1, spans + 1)
    ]
    shard_pair, far_blocks = lax.optimization_barrier((shard_pair, far_blocks))

    def delta_local(out_terms, start_mats, start_vecs):
        local_out, carry_out = block_outputs(*out_terms)
        own_out = local_out + jnp.einsum(
            "hntd,hnde->hnte", carry_out, start_vecs, precision=highest
        )
        reach = jnp.einsum("hntd,hnde->hnte", carry_out, start_mats, precision=highest)
        return own_out, reach

    query_rows = attn_q.reshape(rows_here, local_heads, DH)
    query_pos = position * rows_here + jnp.arange(rows_here, dtype=jnp.int32)
    key_width = attn_k.shape[1]

    def attend(query_rows, key_rows, value_rows, back):
        key_pos = query_pos - back * rows_here
        return window_block(
            query_rows,
            key_rows.reshape(rows_here, local_heads, DH),
            value_rows.reshape(rows_here, local_heads, DH),
            query_pos,
            key_pos,
        )

    def far_attend(query_rows, block, back):
        return attend(query_rows, block[:, :key_width], block[:, key_width:], back)

    def combine(w_attn_out, *parts):
        maxima = [part[0] for part in parts]
        top = maxima[0]
        for block_max in maxima[1:]:
            top = jnp.maximum(top, block_max)
        numer = jnp.zeros_like(parts[0][1])
        denom = jnp.zeros_like(parts[0][2])
        for block_max, block_num, block_den in parts:
            factor = jnp.exp(block_max - top)
            numer = numer + factor[..., None] * block_num
            denom = denom + factor * block_den
        attn_heads = (
            (numer / denom[..., None])
            .transpose(1, 0, 2)
            .reshape(rows_here, local_heads * DH)
            .astype(jnp.bfloat16)
        )
        return jnp.dot(attn_heads, w_attn_out, preferred_element_type=jnp.float32)

    fillers = [
        (delta_local, (out_terms, start_mats, start_vecs)),
        (lambda q, k, v: attend(q, k, v, 0), (query_rows, attn_k, attn_v)),
    ]
    for back in range(1, spans + 1):
        fillers.append(
            (lambda q, blk, back=back: far_attend(q, blk, back), (query_rows, far_blocks[back - 1]))
        )
    incoming_state, results = prefix_state(shard_pair, "ctx", fillers)
    (own_out, reach), attn_parts = results[0], results[1:]
    attn_sum = combine(w_attn_out, *attn_parts)
    delta_raw = own_out + jnp.einsum("hntd,hde->hnte", reach, incoming_state, precision=highest)
    delta_raw = delta_raw.transpose(1, 2, 0, 3).reshape(rows_here, local_heads, DH)
    gate_act = jax.nn.silu(out_gate.astype(jnp.float32).reshape(rows_here, local_heads, DH))
    normed = (
        delta_raw
        / jnp.sqrt(jnp.mean(delta_raw * delta_raw, axis=-1, keepdims=True) + 1e-06)
        * norm_gain
        * gate_act
    )
    delta_heads = normed.reshape(rows_here, local_heads * DH).astype(jnp.bfloat16)
    running_partial_sum = attn_sum + jnp.dot(
        delta_heads, w_delta_out, preferred_element_type=jnp.float32
    )
    n_head = lax.axis_size("head")
    pieces = lax.all_to_all(
        running_partial_sum.astype(jnp.bfloat16), "head", 0, 0, tiled=True
    )
    pieces = pieces.reshape(n_head, rows_here // n_head, pieces.shape[-1]).astype(jnp.float32)
    return jnp.sum(pieces, axis=0).astype(jnp.bfloat16)


def solution(mesh):
    return jax.shard_map(
        shards,
        mesh=mesh,
        in_specs=(
            P("ctx", "head"),
            P("ctx", "head"),
            P("ctx", "head"),
            P("ctx", "head"),
            P("ctx", "head"),
            P("ctx", "head"),
            P(),
            P("ctx", "head"),
            P("ctx", "head"),
            P("ctx", "head"),
            P("head", None),
            P("head", None),
        ),
        out_specs=P(("ctx", "head"), None),
        check_vma=False,
    )
```

```python
import jax
import jax.numpy as jnp
from jax import lax
from jax.sharding import PartitionSpec as P

DH = 128
WINDOW = 1024


highest = lax.Precision.HIGHEST


def prefix_state(pair, axis, fillers):
    place = lax.axis_index(axis)
    size = lax.axis_size(axis)
    total_mat, total_vec = pair
    width = total_mat.shape[-1]
    before_mat = before_vec = None
    done = []
    pending = list(fillers)

    def fill(far, gate):
        if not pending:
            return far
        work, inputs = pending.pop(0)
        inputs, _ = lax.optimization_barrier((inputs, gate))
        result, far = lax.optimization_barrier((work(*inputs), far))
        done.append(result)
        return far

    def apply(mat, far):
        return jnp.einsum("hij,hjk->hik", mat, far, precision=highest)

    bit = 1
    while bit < size:
        upper = (place // bit) % 2 == 1
        if 2 * bit >= size:
            route = [(i, i + bit) for i in range(size) if (i // bit) % 2 == 0]
            far_vec = lax.ppermute(total_vec.astype(jnp.bfloat16), axis, route)
            far_vec = fill(far_vec, total_vec).astype(jnp.float32)
            if before_mat is None:
                before_vec = far_vec
            else:
                before_vec = jnp.where(upper, apply(before_mat, far_vec) + before_vec, before_vec)
        else:
            route = [(i, i ^ bit) for i in range(size)]
            packed = jnp.concatenate([total_mat, total_vec], axis=-1)
            far = lax.ppermute(packed.astype(jnp.bfloat16), axis, route)
            far = fill(far, total_vec).astype(jnp.float32)
            far_mat, far_vec = far[..., :width], far[..., width:]
            joined = apply(
                jnp.where(upper, total_mat, far_mat), jnp.where(upper, far, packed)
            )
            new_mat = joined[..., :width]
            new_vec = joined[..., width:] + jnp.where(upper, total_vec, far_vec)
            if before_mat is None:
                identity = jnp.broadcast_to(jnp.eye(width, dtype=jnp.float32), total_mat.shape)
                before_mat = jnp.where(upper, far_mat, identity)
                before_vec = jnp.where(upper, far_vec, jnp.zeros_like(far_vec))
            else:
                joined = apply(before_mat, far)
                before_mat = jnp.where(upper, joined[..., :width], before_mat)
                before_vec = jnp.where(upper, joined[..., width:] + before_vec, before_vec)
            total_mat, total_vec = new_mat, new_vec
        bit *= 2
    while pending:
        work, inputs = pending.pop(0)
        done.append(work(*inputs))
    return before_vec, done


def passed_along(block, axis, distance):
    devices = range(lax.axis_size(axis))
    route = [(i - distance, i) for i in devices if i - distance in devices]
    return lax.ppermute(block, axis, route)


def unit_rows(array):
    return array / jnp.sqrt(jnp.sum(array * array, axis=-1, keepdims=True) + 1e-06)


def unit_inverse(lower_part):
    order_len = lower_part.shape[-1]
    identity = jnp.eye(order_len, dtype=jnp.float32)
    powered = -lower_part
    result = identity + powered
    for counter in range(1, max(1, (order_len - 1).bit_length())):
        powered = jnp.matmul(powered, powered, precision=highest)
        result = jnp.matmul(result, identity + powered, precision=highest)
    return result


def block_terms(queries, keys_in, values_in, betas, log_rates):
    cumulative = jnp.cumsum(log_rates, axis=-1)
    length = queries.shape[-2]
    positions = jnp.arange(length)
    strict = positions[:, None] > positions[None, :]
    inclusive = positions[:, None] >= positions[None, :]
    spread = cumulative[..., :, None] - cumulative[..., None, :]
    ratio_strict = jnp.where(strict, jnp.exp(jnp.where(strict, spread, 0.0)), 0.0)
    ratio_incl = jnp.where(inclusive, jnp.exp(jnp.where(inclusive, spread, 0.0)), 0.0)
    key_gram = jnp.einsum("...td,...sd->...ts", keys_in, keys_in, precision=highest)
    inverse = unit_inverse(betas[..., :, None] * ratio_strict * key_gram)
    decayed = jnp.exp(cumulative)
    pseudo = jnp.matmul(inverse, betas[..., None] * values_in, precision=highest)
    writer = jnp.matmul(inverse, (betas * decayed)[..., None] * keys_in, precision=highest)
    to_end = jnp.exp(cumulative[..., -1:] - cumulative)
    keys_end = keys_in * to_end[..., None]
    identity = jnp.eye(queries.shape[-1], dtype=jnp.float32)
    transition = jnp.exp(cumulative[..., -1])[..., None, None] * identity - jnp.einsum(
        "...td,...te->...de", keys_end, writer, precision=highest
    )
    contrib = jnp.einsum("...td,...te->...de", keys_end, pseudo, precision=highest)
    return (transition, contrib, (queries, keys_in, ratio_incl, decayed, pseudo, writer))


def block_outputs(queries, keys_in, ratio_incl, decayed, pseudo, writer):
    mixing = ratio_incl * jnp.einsum("...td,...sd->...ts", queries, keys_in, precision=highest)
    local_out = jnp.matmul(mixing, pseudo, precision=highest)
    carry_out = decayed[..., None] * queries - jnp.matmul(mixing, writer, precision=highest)
    return (local_out, carry_out)


def window_block(queries, keys_in, values_in, query_pos, key_pos):
    scores = jnp.einsum(
        "thd,shd->hts", queries, keys_in, preferred_element_type=jnp.float32
    ) * DH ** (-0.5)
    offsets = query_pos[:, None] - key_pos[None, :]
    inside = (offsets >= 0) & (offsets < WINDOW) & (key_pos[None, :] >= 0)
    masked = jnp.where(inside[None], scores, -1e30)
    block_max = jnp.max(masked, axis=-1)
    weights = jnp.where(inside[None], jnp.exp(masked - block_max[..., None]), 0.0)
    probs = weights.astype(jnp.bfloat16)
    block_num = jnp.einsum("hts,shd->htd", probs, values_in, preferred_element_type=jnp.float32)
    block_den = jnp.sum(weights, axis=-1)
    return (block_max, block_num, block_den)


def chain_pairs(earlier, later):
    matrix = jnp.einsum("hij,hjk->hik", later[0], earlier[0], precision=highest)
    vector = jnp.einsum("hij,hjk->hik", later[0], earlier[1], precision=highest) + later[1]
    return (matrix, vector)


def shards(
    delta_q,
    delta_k,
    delta_v,
    beta,
    log_decay,
    out_gate,
    norm_gain,
    attn_q,
    attn_k,
    attn_v,
    w_delta_out,
    w_attn_out,
):
    rows_here = delta_q.shape[0]
    local_heads = delta_q.shape[1] // DH
    block_len = min(64, rows_here)
    blocks = rows_here // block_len

    def heads_blocks(array):
        return (
            array.astype(jnp.float32)
            .reshape(blocks, block_len, local_heads, DH)
            .transpose(2, 0, 1, 3)
        )

    queries = unit_rows(heads_blocks(delta_q)) * DH ** (-0.5)
    keys_in = unit_rows(heads_blocks(delta_k))
    values_in = heads_blocks(delta_v)
    betas = beta.reshape(blocks, block_len, local_heads).transpose(2, 0, 1)
    log_rates = log_decay.reshape(blocks, block_len, local_heads).transpose(2, 0, 1)
    transition, contrib, out_terms = block_terms(queries, keys_in, values_in, betas, log_rates)
    identity = jnp.broadcast_to(jnp.eye(DH, dtype=jnp.float32), (local_heads, DH, DH))
    zero_state = jnp.zeros((local_heads, DH, DH), jnp.float32)
    start_mats = [identity]
    start_vecs = [zero_state]
    run_mat, run_vec = transition[:, 0], contrib[:, 0]
    for block in range(1, blocks):
        start_mats.append(run_mat)
        start_vecs.append(run_vec)
        joined = jnp.einsum(
            "hij,hjk->hik",
            transition[:, block],
            jnp.concatenate([run_mat, run_vec], axis=-1),
            precision=highest,
        )
        run_mat = joined[..., :DH]
        run_vec = joined[..., DH:] + contrib[:, block]
    shard_pair = (run_mat, run_vec)
    position = lax.axis_index("ctx")
    spans = WINDOW // rows_here
    far_blocks = [
        passed_along(jnp.concatenate([attn_k, attn_v], axis=-1), "ctx", back)
        for back in range(1, spans + 1)
    ]
    shard_pair, far_blocks = lax.optimization_barrier((shard_pair, far_blocks))

    def delta_local(out_terms, start_mats, start_vecs):
        start_mats = jnp.stack(start_mats, axis=1)
        start_vecs = jnp.stack(start_vecs, axis=1)
        local_out, carry_out = block_outputs(*out_terms)
        own_out = local_out + jnp.einsum(
            "hntd,hnde->hnte", carry_out, start_vecs, precision=highest
        )
        reach = jnp.einsum("hntd,hnde->hnte", carry_out, start_mats, precision=highest)
        return own_out, reach

    key_width = attn_k.shape[1]

    def attend(query_rows, key_rows, value_rows, back):
        query_pos = position * rows_here + jnp.arange(rows_here, dtype=jnp.int32)
        key_pos = query_pos - back * rows_here
        return window_block(
            query_rows.reshape(rows_here, local_heads, DH),
            key_rows.reshape(rows_here, local_heads, DH),
            value_rows.reshape(rows_here, local_heads, DH),
            query_pos,
            key_pos,
        )

    def far_attend(query_rows, block, back):
        return attend(query_rows, block[:, :key_width], block[:, key_width:], back)

    def combine(w_attn_out, *parts):
        maxima = [part[0] for part in parts]
        top = maxima[0]
        for block_max in maxima[1:]:
            top = jnp.maximum(top, block_max)
        numer = jnp.zeros_like(parts[0][1])
        denom = jnp.zeros_like(parts[0][2])
        for block_max, block_num, block_den in parts:
            factor = jnp.exp(block_max - top)
            numer = numer + factor[..., None] * block_num
            denom = denom + factor * block_den
        attn_heads = (
            (numer / denom[..., None])
            .transpose(1, 0, 2)
            .reshape(rows_here, local_heads * DH)
            .astype(jnp.bfloat16)
        )
        return jnp.dot(attn_heads, w_attn_out, preferred_element_type=jnp.float32)

    fillers = [
        (delta_local, (out_terms, start_mats, start_vecs)),
        (lambda q, k, v: attend(q, k, v, 0), (attn_q, attn_k, attn_v)),
    ]
    for back in range(1, spans + 1):
        fillers.append(
            (lambda q, blk, back=back: far_attend(q, blk, back), (attn_q, far_blocks[back - 1]))
        )
    incoming_state, results = prefix_state(shard_pair, "ctx", fillers)
    (own_out, reach), attn_parts = results[0], results[1:]
    attn_sum = combine(w_attn_out, *attn_parts)
    delta_raw = own_out + jnp.einsum("hntd,hde->hnte", reach, incoming_state, precision=highest)
    delta_raw = delta_raw.transpose(1, 2, 0, 3).reshape(rows_here, local_heads, DH)
    gate_act = jax.nn.silu(out_gate.astype(jnp.float32).reshape(rows_here, local_heads, DH))
    normed = (
        delta_raw
        / jnp.sqrt(jnp.mean(delta_raw * delta_raw, axis=-1, keepdims=True) + 1e-06)
        * norm_gain
        * gate_act
    )
    delta_heads = normed.reshape(rows_here, local_heads * DH).astype(jnp.bfloat16)
    running_partial_sum = attn_sum + jnp.dot(
        delta_heads, w_delta_out, preferred_element_type=jnp.float32
    )
    n_head = lax.axis_size("head")
    pieces = lax.all_to_all(
        running_partial_sum.astype(jnp.bfloat16), "head", 0, 0, tiled=True
    )
    pieces = pieces.reshape(n_head, rows_here // n_head, pieces.shape[-1]).astype(jnp.float32)
    return jnp.sum(pieces, axis=0).astype(jnp.bfloat16)


def solution(mesh):
    return jax.shard_map(
        shards,
        mesh=mesh,
        in_specs=(
            P("ctx", "head"),
            P("ctx", "head"),
            P("ctx", "head"),
            P("ctx", "head"),
            P("ctx", "head"),
            P("ctx", "head"),
            P(),
            P("ctx", "head"),
            P("ctx", "head"),
            P("ctx", "head"),
            P("head", None),
            P("head", None),
        ),
        out_specs=P(("ctx", "head"), None),
        check_vma=False,
    )
```

```python
import jax
import jax.numpy as jnp
from jax import lax
from jax.sharding import PartitionSpec as P

DH = 128
WINDOW = 1024


highest = lax.Precision.HIGHEST


def prefix_state(pair, axis, fillers):
    place = lax.axis_index(axis)
    size = lax.axis_size(axis)
    first_mat, first_vec = pair
    heads, width = first_mat.shape[0], first_mat.shape[-1]
    half = heads // 2
    done = []
    pending = list(fillers)

    def fill(far, gate):
        if not pending:
            return far
        work, inputs = pending.pop(0)
        inputs, _ = lax.optimization_barrier((inputs, gate))
        result, far = lax.optimization_barrier((work(*inputs), far))
        done.append(result)
        return far

    def apply(mat, far):
        return jnp.einsum("hij,hjk->hik", mat, far, precision=highest)

    def swap(array, bit):
        route = [(i, i ^ bit) for i in range(size)]
        return lax.ppermute(array.astype(jnp.bfloat16), axis, route)

    odd = place % 2 == 1
    packed = jnp.concatenate([first_mat, first_vec], axis=-1)
    pair_far = fill(swap(packed, 1), first_vec).astype(jnp.float32)
    joined = apply(jnp.where(odd, first_mat, pair_far[..., :width]), jnp.where(odd, pair_far, packed))
    total = joined.at[..., width:].add(jnp.where(odd, first_vec, pair_far[..., width:]))
    total = lax.dynamic_slice_in_dim(total, (place % 2) * half, half, 0)
    total_mat, total_vec = total[..., :width], total[..., width:]
    before_mat = before_vec = None
    bit = 2
    while bit < size:
        upper = (place // bit) % 2 == 1
        if 2 * bit >= size:
            route = [(i, i + bit) for i in range(size) if (i // bit) % 2 == 0]
            far_vec = lax.ppermute(total_vec.astype(jnp.bfloat16), axis, route)
            far_vec = fill(far_vec, total_vec).astype(jnp.float32)
            if before_mat is None:
                before_vec = far_vec
            else:
                before_vec = jnp.where(upper, apply(before_mat, far_vec) + before_vec, before_vec)
        else:
            packed = jnp.concatenate([total_mat, total_vec], axis=-1)
            far = fill(swap(packed, bit), total_vec).astype(jnp.float32)
            far_mat, far_vec = far[..., :width], far[..., width:]
            joined = apply(jnp.where(upper, total_mat, far_mat), jnp.where(upper, far, packed))
            new_mat = joined[..., :width]
            new_vec = joined[..., width:] + jnp.where(upper, total_vec, far_vec)
            if before_mat is None:
                identity = jnp.broadcast_to(jnp.eye(width, dtype=jnp.float32), total_mat.shape)
                before_mat = jnp.where(upper, far_mat, identity)
                before_vec = jnp.where(upper, far_vec, jnp.zeros_like(far_vec))
            else:
                joined = apply(before_mat, far)
                before_mat = jnp.where(upper, joined[..., :width], before_mat)
                before_vec = jnp.where(upper, joined[..., width:] + before_vec, before_vec)
            total_mat, total_vec = new_mat, new_vec
        bit *= 2
    other = fill(swap(before_vec, 1), before_vec).astype(jnp.float32)
    entering = jnp.where(
        odd,
        jnp.concatenate([other, before_vec], axis=0),
        jnp.concatenate([before_vec, other], axis=0),
    )
    entering = jnp.where(
        odd, apply(pair_far[..., :width], entering) + pair_far[..., width:], entering
    )
    while pending:
        work, inputs = pending.pop(0)
        done.append(work(*inputs))
    return entering, done


def passed_along(block, axis, distance):
    devices = range(lax.axis_size(axis))
    route = [(i - distance, i) for i in devices if i - distance in devices]
    return lax.ppermute(block, axis, route)


def unit_rows(array):
    return array / jnp.sqrt(jnp.sum(array * array, axis=-1, keepdims=True) + 1e-06)


def unit_inverse(lower_part):
    order_len = lower_part.shape[-1]
    identity = jnp.eye(order_len, dtype=jnp.float32)
    powered = -lower_part
    result = identity + powered
    for counter in range(1, max(1, (order_len - 1).bit_length())):
        powered = jnp.matmul(powered, powered, precision=highest)
        result = jnp.matmul(result, identity + powered, precision=highest)
    return result


def block_terms(keys_in, values_in, betas, log_rates):
    cumulative = jnp.cumsum(log_rates, axis=-1)
    length = keys_in.shape[-2]
    positions = jnp.arange(length)
    strict = positions[:, None] > positions[None, :]
    inclusive = positions[:, None] >= positions[None, :]
    spread = cumulative[..., :, None] - cumulative[..., None, :]
    ratio_strict = jnp.where(strict, jnp.exp(jnp.where(strict, spread, 0.0)), 0.0)
    key_gram = jnp.einsum("...td,...sd->...ts", keys_in, keys_in, precision=highest)
    inverse = unit_inverse(betas[..., :, None] * ratio_strict * key_gram)
    decayed = jnp.exp(cumulative)
    pseudo = jnp.matmul(inverse, betas[..., None] * values_in, precision=highest)
    writer = jnp.matmul(inverse, (betas * decayed)[..., None] * keys_in, precision=highest)
    to_end = jnp.exp(cumulative[..., -1:] - cumulative)
    keys_end = keys_in * to_end[..., None]
    identity = jnp.eye(keys_in.shape[-1], dtype=jnp.float32)
    transition = jnp.exp(cumulative[..., -1])[..., None, None] * identity - jnp.einsum(
        "...td,...te->...de", keys_end, writer, precision=highest
    )
    contrib = jnp.einsum("...td,...te->...de", keys_end, pseudo, precision=highest)
    return (transition, contrib, (keys_in, cumulative, decayed, pseudo, writer))


def block_outputs(queries, keys_in, cumulative, decayed, pseudo, writer):
    positions = jnp.arange(keys_in.shape[-2])
    inclusive = positions[:, None] >= positions[None, :]
    spread = cumulative[..., :, None] - cumulative[..., None, :]
    ratio_incl = jnp.where(inclusive, jnp.exp(jnp.where(inclusive, spread, 0.0)), 0.0)
    mixing = ratio_incl * jnp.einsum("...td,...sd->...ts", queries, keys_in, precision=highest)
    local_out = jnp.matmul(mixing, pseudo, precision=highest)
    carry_out = decayed[..., None] * queries - jnp.matmul(mixing, writer, precision=highest)
    return (local_out, carry_out)


def window_block(queries, keys_in, values_in, query_pos, key_pos):
    scores = jnp.einsum(
        "thd,shd->hts", queries, keys_in, preferred_element_type=jnp.float32
    ) * DH ** (-0.5)
    offsets = query_pos[:, None] - key_pos[None, :]
    inside = (offsets >= 0) & (offsets < WINDOW) & (key_pos[None, :] >= 0)
    masked = jnp.where(inside[None], scores, -1e30)
    block_max = jnp.max(masked, axis=-1)
    weights = jnp.where(inside[None], jnp.exp(masked - block_max[..., None]), 0.0)
    probs = weights.astype(jnp.bfloat16)
    block_num = jnp.einsum("hts,shd->htd", probs, values_in, preferred_element_type=jnp.float32)
    block_den = jnp.sum(weights, axis=-1)
    return (block_max, block_num, block_den)


def chain_pairs(earlier, later):
    matrix = jnp.einsum("hij,hjk->hik", later[0], earlier[0], precision=highest)
    vector = jnp.einsum("hij,hjk->hik", later[0], earlier[1], precision=highest) + later[1]
    return (matrix, vector)


def shards(
    delta_q,
    delta_k,
    delta_v,
    beta,
    log_decay,
    out_gate,
    norm_gain,
    attn_q,
    attn_k,
    attn_v,
    w_delta_out,
    w_attn_out,
):
    rows_here = delta_q.shape[0]
    local_heads = delta_q.shape[1] // DH
    block_len = min(64, rows_here)
    blocks = rows_here // block_len

    def heads_blocks(array):
        return (
            array.astype(jnp.float32)
            .reshape(blocks, block_len, local_heads, DH)
            .transpose(2, 0, 1, 3)
        )

    keys_in = unit_rows(heads_blocks(delta_k))
    values_in = heads_blocks(delta_v)
    betas = beta.reshape(blocks, block_len, local_heads).transpose(2, 0, 1)
    log_rates = log_decay.reshape(blocks, block_len, local_heads).transpose(2, 0, 1)
    transition, contrib, out_terms = block_terms(keys_in, values_in, betas, log_rates)
    identity = jnp.broadcast_to(jnp.eye(DH, dtype=jnp.float32), (local_heads, DH, DH))
    zero_state = jnp.zeros((local_heads, DH, DH), jnp.float32)
    start_mats = [identity]
    start_vecs = [zero_state]
    run_mat, run_vec = transition[:, 0], contrib[:, 0]
    for block in range(1, blocks):
        start_mats.append(run_mat)
        start_vecs.append(run_vec)
        joined = jnp.einsum(
            "hij,hjk->hik",
            transition[:, block],
            jnp.concatenate([run_mat, run_vec], axis=-1),
            precision=highest,
        )
        run_mat = joined[..., :DH]
        run_vec = joined[..., DH:] + contrib[:, block]
    shard_pair = (run_mat, run_vec)
    position = lax.axis_index("ctx")
    spans = WINDOW // rows_here
    far_blocks = [
        passed_along(jnp.concatenate([attn_k, attn_v], axis=-1), "ctx", back)
        for back in range(1, spans + 1)
    ]
    shard_pair, far_blocks = lax.optimization_barrier((shard_pair, far_blocks))

    def delta_local(delta_q, out_terms, start_mats, start_vecs):
        start_mats = jnp.stack(start_mats, axis=1)
        start_vecs = jnp.stack(start_vecs, axis=1)
        queries = unit_rows(heads_blocks(delta_q)) * DH ** (-0.5)
        local_out, carry_out = block_outputs(queries, *out_terms)
        own_out = local_out + jnp.einsum(
            "hntd,hnde->hnte", carry_out, start_vecs, precision=highest
        )
        reach = jnp.einsum("hntd,hnde->hnte", carry_out, start_mats, precision=highest)
        return own_out, reach

    key_width = attn_k.shape[1]

    def attend(query_rows, key_rows, value_rows, back):
        query_pos = position * rows_here + jnp.arange(rows_here, dtype=jnp.int32)
        key_pos = query_pos - back * rows_here
        return window_block(
            query_rows.reshape(rows_here, local_heads, DH),
            key_rows.reshape(rows_here, local_heads, DH),
            value_rows.reshape(rows_here, local_heads, DH),
            query_pos,
            key_pos,
        )

    def far_attend(query_rows, block, back):
        return attend(query_rows, block[:, :key_width], block[:, key_width:], back)

    def combine(w_attn_out, *parts):
        maxima = [part[0] for part in parts]
        top = maxima[0]
        for block_max in maxima[1:]:
            top = jnp.maximum(top, block_max)
        numer = jnp.zeros_like(parts[0][1])
        denom = jnp.zeros_like(parts[0][2])
        for block_max, block_num, block_den in parts:
            factor = jnp.exp(block_max - top)
            numer = numer + factor[..., None] * block_num
            denom = denom + factor * block_den
        attn_heads = (
            (numer / denom[..., None])
            .transpose(1, 0, 2)
            .reshape(rows_here, local_heads * DH)
            .astype(jnp.bfloat16)
        )
        return jnp.dot(attn_heads, w_attn_out, preferred_element_type=jnp.float32)

    fillers = [
        (delta_local, (delta_q, out_terms, start_mats, start_vecs)),
        (lambda q, k, v: attend(q, k, v, 0), (attn_q, attn_k, attn_v)),
    ]
    for back in range(1, spans + 1):
        fillers.append(
            (lambda q, blk, back=back: far_attend(q, blk, back), (attn_q, far_blocks[back - 1]))
        )
    incoming_state, results = prefix_state(shard_pair, "ctx", fillers)
    (own_out, reach), attn_parts = results[0], results[1:]
    attn_sum = combine(w_attn_out, *attn_parts)
    delta_raw = own_out + jnp.einsum("hntd,hde->hnte", reach, incoming_state, precision=highest)
    delta_raw = delta_raw.transpose(1, 2, 0, 3).reshape(rows_here, local_heads, DH)
    gate_act = jax.nn.silu(out_gate.astype(jnp.float32).reshape(rows_here, local_heads, DH))
    normed = (
        delta_raw
        / jnp.sqrt(jnp.mean(delta_raw * delta_raw, axis=-1, keepdims=True) + 1e-06)
        * norm_gain
        * gate_act
    )
    delta_heads = normed.reshape(rows_here, local_heads * DH).astype(jnp.bfloat16)
    running_partial_sum = attn_sum + jnp.dot(
        delta_heads, w_delta_out, preferred_element_type=jnp.float32
    )
    n_head = lax.axis_size("head")
    pieces = lax.all_to_all(
        running_partial_sum.astype(jnp.bfloat16), "head", 0, 0, tiled=True
    )
    pieces = pieces.reshape(n_head, rows_here // n_head, pieces.shape[-1]).astype(jnp.float32)
    return jnp.sum(pieces, axis=0).astype(jnp.bfloat16)


def solution(mesh):
    return jax.shard_map(
        shards,
        mesh=mesh,
        in_specs=(
            P("ctx", "head"),
            P("ctx", "head"),
            P("ctx", "head"),
            P("ctx", "head"),
            P("ctx", "head"),
            P("ctx", "head"),
            P(),
            P("ctx", "head"),
            P("ctx", "head"),
            P("ctx", "head"),
            P("head", None),
            P("head", None),
        ),
        out_specs=P(("ctx", "head"), None),
        check_vma=False,
    )
```

```python
import jax
import jax.numpy as jnp
from jax import lax
from jax.sharding import PartitionSpec as P

DH = 128
WINDOW = 1024


highest = lax.Precision.HIGHEST


def prefix_state(pair, axis, fillers):
    place = lax.axis_index(axis)
    size = lax.axis_size(axis)
    first_mat, first_vec = pair
    heads, width = first_mat.shape[0], first_mat.shape[-1]
    half = heads // 2
    done = []
    pending = list(fillers)

    def fill(far, gate):
        if not pending:
            return far
        item = pending.pop(0)
        if item is None:
            done.append(None)
            return far
        work, inputs, tie = item
        inputs, _ = lax.optimization_barrier((inputs(done), gate))
        result = work(*inputs)
        if tie:
            result, far = lax.optimization_barrier((result, far))
        done.append(result)
        return far

    def apply(mat, far):
        return jnp.einsum("hij,hjk->hik", mat, far, precision=highest)

    def swap(array, bit):
        route = [(i, i ^ bit) for i in range(size)]
        return lax.ppermute(array.astype(jnp.bfloat16), axis, route)

    odd = place % 2 == 1
    packed = jnp.concatenate([first_mat, first_vec], axis=-1)
    pair_far = fill(swap(packed, 1), first_vec).astype(jnp.float32)
    joined = apply(jnp.where(odd, first_mat, pair_far[..., :width]), jnp.where(odd, pair_far, packed))
    total = joined.at[..., width:].add(jnp.where(odd, first_vec, pair_far[..., width:]))
    total = lax.dynamic_slice_in_dim(total, (place % 2) * half, half, 0)
    total_mat, total_vec = total[..., :width], total[..., width:]
    before_mat = before_vec = None
    bit = 2
    while bit < size:
        upper = (place // bit) % 2 == 1
        if 2 * bit >= size:
            route = [(i, i + bit) for i in range(size) if (i // bit) % 2 == 0]
            far_vec = lax.ppermute(total_vec.astype(jnp.bfloat16), axis, route)
            far_vec = fill(far_vec, total_vec).astype(jnp.float32)
            if before_mat is None:
                before_vec = far_vec
            else:
                before_vec = jnp.where(upper, apply(before_mat, far_vec) + before_vec, before_vec)
        else:
            packed = jnp.concatenate([total_mat, total_vec], axis=-1)
            far = fill(swap(packed, bit), total_vec).astype(jnp.float32)
            far_mat, far_vec = far[..., :width], far[..., width:]
            joined = apply(jnp.where(upper, total_mat, far_mat), jnp.where(upper, far, packed))
            new_mat = joined[..., :width]
            new_vec = joined[..., width:] + jnp.where(upper, total_vec, far_vec)
            if before_mat is None:
                identity = jnp.broadcast_to(jnp.eye(width, dtype=jnp.float32), total_mat.shape)
                before_mat = jnp.where(upper, far_mat, identity)
                before_vec = jnp.where(upper, far_vec, jnp.zeros_like(far_vec))
            else:
                joined = apply(before_mat, far)
                before_mat = jnp.where(upper, joined[..., :width], before_mat)
                before_vec = jnp.where(upper, joined[..., width:] + before_vec, before_vec)
            total_mat, total_vec = new_mat, new_vec
        bit *= 2
    other = fill(swap(before_vec, 1), before_vec).astype(jnp.float32)
    entering = jnp.where(
        odd,
        jnp.concatenate([other, before_vec], axis=0),
        jnp.concatenate([before_vec, other], axis=0),
    )
    entering = jnp.where(
        odd, apply(pair_far[..., :width], entering) + pair_far[..., width:], entering
    )
    while pending:
        item = pending.pop(0)
        done.append(None if item is None else item[0](*item[1](done)))
    return entering, done


def passed_along(block, axis, distance):
    devices = range(lax.axis_size(axis))
    route = [(i - distance, i) for i in devices if i - distance in devices]
    return lax.ppermute(block, axis, route)


def unit_rows(array):
    return array / jnp.sqrt(jnp.sum(array * array, axis=-1, keepdims=True) + 1e-06)


def unit_inverse(lower_part):
    order_len = lower_part.shape[-1]
    identity = jnp.eye(order_len, dtype=jnp.float32)
    power = -lower_part
    total = identity + power
    steps = max(1, (order_len - 1).bit_length())
    if steps > 1:
        power = jnp.matmul(power, power, precision=highest)
    for counter in range(2, steps):
        both = jnp.matmul(
            jnp.stack([total, power]), jnp.stack([identity + power, power]), precision=highest
        )
        total, power = both[0], both[1]
    if steps > 1:
        total = jnp.matmul(total, identity + power, precision=highest)
    return total


def block_terms(keys_in, values_in, betas, log_rates):
    cumulative = jnp.cumsum(log_rates, axis=-1)
    length = keys_in.shape[-2]
    positions = jnp.arange(length)
    strict = positions[:, None] > positions[None, :]
    inclusive = positions[:, None] >= positions[None, :]
    spread = cumulative[..., :, None] - cumulative[..., None, :]
    ratio_strict = jnp.where(strict, jnp.exp(jnp.where(strict, spread, 0.0)), 0.0)
    key_gram = jnp.einsum("...td,...sd->...ts", keys_in, keys_in, precision=highest)
    inverse = unit_inverse(betas[..., :, None] * ratio_strict * key_gram)
    decayed = jnp.exp(cumulative)
    pseudo = jnp.matmul(inverse, betas[..., None] * values_in, precision=highest)
    writer = jnp.matmul(inverse, (betas * decayed)[..., None] * keys_in, precision=highest)
    to_end = jnp.exp(cumulative[..., -1:] - cumulative)
    keys_end = keys_in * to_end[..., None]
    identity = jnp.eye(keys_in.shape[-1], dtype=jnp.float32)
    transition = jnp.exp(cumulative[..., -1])[..., None, None] * identity - jnp.einsum(
        "...td,...te->...de", keys_end, writer, precision=highest
    )
    contrib = jnp.einsum("...td,...te->...de", keys_end, pseudo, precision=highest)
    return (transition, contrib, (keys_in, cumulative, decayed, pseudo, writer))


def block_outputs(queries, keys_in, cumulative, decayed, pseudo, writer):
    positions = jnp.arange(keys_in.shape[-2])
    inclusive = positions[:, None] >= positions[None, :]
    spread = cumulative[..., :, None] - cumulative[..., None, :]
    ratio_incl = jnp.where(inclusive, jnp.exp(jnp.where(inclusive, spread, 0.0)), 0.0)
    mixing = ratio_incl * jnp.einsum("...td,...sd->...ts", queries, keys_in, precision=highest)
    local_out = jnp.matmul(mixing, pseudo, precision=highest)
    carry_out = decayed[..., None] * queries - jnp.matmul(mixing, writer, precision=highest)
    return (local_out, carry_out)


def window_block(queries, keys_in, values_in, query_pos, key_pos):
    scores = jnp.einsum(
        "thd,shd->hts", queries, keys_in, preferred_element_type=jnp.float32
    ) * DH ** (-0.5)
    offsets = query_pos[:, None] - key_pos[None, :]
    inside = (offsets >= 0) & (offsets < WINDOW) & (key_pos[None, :] >= 0)
    masked = jnp.where(inside[None], scores, -1e30)
    block_max = jnp.max(masked, axis=-1)
    weights = jnp.where(inside[None], jnp.exp(masked - block_max[..., None]), 0.0)
    probs = weights.astype(jnp.bfloat16)
    block_num = jnp.einsum("hts,shd->htd", probs, values_in, preferred_element_type=jnp.float32)
    block_den = jnp.sum(weights, axis=-1)
    return (block_max, block_num, block_den)


def window_blocks(queries, keys_in, values_in, query_pos, key_pos):
    scores = jnp.einsum(
        "thd,bshd->bhts", queries, keys_in, preferred_element_type=jnp.float32
    ) * DH ** (-0.5)
    offsets = query_pos[None, :, None] - key_pos[:, None, :]
    inside = (offsets >= 0) & (offsets < WINDOW) & (key_pos[:, None, :] >= 0)
    masked = jnp.where(inside[:, None], scores, -1e30)
    block_max = jnp.max(masked, axis=-1)
    weights = jnp.where(inside[:, None], jnp.exp(masked - block_max[..., None]), 0.0)
    probs = weights.astype(jnp.bfloat16)
    block_num = jnp.einsum("bhts,bshd->bhtd", probs, values_in, preferred_element_type=jnp.float32)
    block_den = jnp.sum(weights, axis=-1)
    return (block_max, block_num, block_den)


def chain_pairs(earlier, later):
    matrix = jnp.einsum("hij,hjk->hik", later[0], earlier[0], precision=highest)
    vector = jnp.einsum("hij,hjk->hik", later[0], earlier[1], precision=highest) + later[1]
    return (matrix, vector)


def shards(
    delta_q,
    delta_k,
    delta_v,
    beta,
    log_decay,
    out_gate,
    norm_gain,
    attn_q,
    attn_k,
    attn_v,
    w_delta_out,
    w_attn_out,
):
    rows_here = delta_q.shape[0]
    local_heads = delta_q.shape[1] // DH
    block_len = min(64, rows_here)
    blocks = rows_here // block_len

    def heads_blocks(array):
        return (
            array.astype(jnp.float32)
            .reshape(blocks, block_len, local_heads, DH)
            .transpose(2, 0, 1, 3)
        )

    keys_in = unit_rows(heads_blocks(delta_k))
    values_in = heads_blocks(delta_v)
    betas = beta.reshape(blocks, block_len, local_heads).transpose(2, 0, 1)
    log_rates = log_decay.reshape(blocks, block_len, local_heads).transpose(2, 0, 1)
    transition, contrib, out_terms = block_terms(keys_in, values_in, betas, log_rates)
    identity = jnp.broadcast_to(jnp.eye(DH, dtype=jnp.float32), (local_heads, DH, DH))
    zero_state = jnp.zeros((local_heads, DH, DH), jnp.float32)
    start_mats = [identity]
    start_vecs = [zero_state]
    run_mat, run_vec = transition[:, 0], contrib[:, 0]
    for block in range(1, blocks):
        start_mats.append(run_mat)
        start_vecs.append(run_vec)
        joined = jnp.einsum(
            "hij,hjk->hik",
            transition[:, block],
            jnp.concatenate([run_mat, run_vec], axis=-1),
            precision=highest,
        )
        run_mat = joined[..., :DH]
        run_vec = joined[..., DH:] + contrib[:, block]
    shard_pair = (run_mat, run_vec)
    position = lax.axis_index("ctx")
    spans = WINDOW // rows_here

    def delta_local(delta_q, out_terms, start_mats, start_vecs):
        start_mats = jnp.stack(start_mats, axis=1)
        start_vecs = jnp.stack(start_vecs, axis=1)
        queries = unit_rows(heads_blocks(delta_q)) * DH ** (-0.5)
        local_out, carry_out = block_outputs(queries, *out_terms)
        own_out = local_out + jnp.einsum(
            "hntd,hnde->hnte", carry_out, start_vecs, precision=highest
        )
        reach = jnp.einsum("hntd,hnde->hnte", carry_out, start_mats, precision=highest)
        return own_out, reach

    key_width = attn_k.shape[1]

    def own_attend(place, query_rows, key_rows, value_rows):
        query_pos = place * rows_here + jnp.arange(rows_here, dtype=jnp.int32)
        return window_block(
            query_rows.reshape(rows_here, local_heads, DH),
            key_rows.reshape(rows_here, local_heads, DH),
            value_rows.reshape(rows_here, local_heads, DH),
            query_pos,
            query_pos,
        )

    def send_back(keys_values):
        return [passed_along(keys_values, "ctx", back) for back in range(1, spans + 1)]

    def far_attend(place, query_rows, far_blocks):
        query_pos = place * rows_here + jnp.arange(rows_here, dtype=jnp.int32)
        backs = jnp.arange(1, spans + 1, dtype=jnp.int32)
        key_pos = query_pos[None, :] - backs[:, None] * rows_here
        stacked = jnp.stack(far_blocks).reshape(spans, rows_here, 2, local_heads, DH)
        return window_blocks(
            query_rows.reshape(rows_here, local_heads, DH),
            stacked[:, :, 0],
            stacked[:, :, 1],
            query_pos,
            key_pos,
        )

    def combine(w_attn_out, own, far):
        parts = [own] + [tuple(item[b] for item in far) for b in range(spans)]
        maxima = [part[0] for part in parts]
        top = maxima[0]
        for block_max in maxima[1:]:
            top = jnp.maximum(top, block_max)
        numer = jnp.zeros_like(parts[0][1])
        denom = jnp.zeros_like(parts[0][2])
        for block_max, block_num, block_den in parts:
            factor = jnp.exp(block_max - top)
            numer = numer + factor[..., None] * block_num
            denom = denom + factor * block_den
        attn_heads = (
            (numer / denom[..., None])
            .transpose(1, 0, 2)
            .reshape(rows_here, local_heads * DH)
            .astype(jnp.bfloat16)
        )
        return jnp.dot(attn_heads, w_attn_out, preferred_element_type=jnp.float32)

    keys_values = jnp.concatenate(
        [attn_k.reshape(rows_here, 1, key_width), attn_v.reshape(rows_here, 1, key_width)], axis=1
    ).reshape(rows_here, 2 * key_width)
    fillers = [
        (delta_local, lambda done: (delta_q, out_terms, start_mats, start_vecs), True),
        (own_attend, lambda done: (position, attn_q, attn_k, attn_v), True),
        (send_back, lambda done: (keys_values,), False),
        None,
        (far_attend, lambda done: (position, attn_q, done[2]), True),
        (combine, lambda done: (w_attn_out, done[1], done[4]), True),
    ]
    incoming_state, results = prefix_state(shard_pair, "ctx", fillers)
    own_out, reach = results[0]
    attn_sum = results[-1]
    delta_raw = own_out + jnp.einsum("hntd,hde->hnte", reach, incoming_state, precision=highest)
    delta_raw = delta_raw.transpose(1, 2, 0, 3).reshape(rows_here, local_heads, DH)
    gate_act = jax.nn.silu(out_gate.astype(jnp.float32).reshape(rows_here, local_heads, DH))
    normed = (
        delta_raw
        / jnp.sqrt(jnp.mean(delta_raw * delta_raw, axis=-1, keepdims=True) + 1e-06)
        * norm_gain
        * gate_act
    )
    delta_heads = normed.reshape(rows_here, local_heads * DH).astype(jnp.bfloat16)
    running_partial_sum = attn_sum + jnp.dot(
        delta_heads, w_delta_out, preferred_element_type=jnp.float32
    )
    n_head = lax.axis_size("head")
    pieces = lax.all_to_all(
        running_partial_sum.astype(jnp.bfloat16), "head", 0, 0, tiled=True
    )
    pieces = pieces.reshape(n_head, rows_here // n_head, pieces.shape[-1]).astype(jnp.float32)
    return jnp.sum(pieces, axis=0).astype(jnp.bfloat16)


def solution(mesh):
    return jax.shard_map(
        shards,
        mesh=mesh,
        in_specs=(
            P("ctx", "head"),
            P("ctx", "head"),
            P("ctx", "head"),
            P("ctx", "head"),
            P("ctx", "head"),
            P("ctx", "head"),
            P(),
            P("ctx", "head"),
            P("ctx", "head"),
            P("ctx", "head"),
            P("head", None),
            P("head", None),
        ),
        out_specs=P(("ctx", "head"), None),
        check_vma=False,
    )
```

```python
import jax
import jax.numpy as jnp
from jax import lax
from jax.sharding import PartitionSpec as P

DH = 128
WINDOW = 1024


highest = lax.Precision.HIGHEST


def prefix_state(pair, axis, fillers):
    place = lax.axis_index(axis)
    size = lax.axis_size(axis)
    first_mat, first_vec = pair
    heads, width = first_mat.shape[0], first_mat.shape[-1]
    half = heads // 2
    done = []
    pending = list(fillers)

    def fill(far, gate):
        if not pending:
            return far
        work, inputs = pending.pop(0)
        inputs, _ = lax.optimization_barrier((inputs, gate))
        result, far = lax.optimization_barrier((work(*inputs), far))
        done.append(result)
        return far

    def apply(mat, far):
        return jnp.einsum("hij,hjk->hik", mat, far, precision=highest)

    def swap(array, bit):
        route = [(i, i ^ bit) for i in range(size)]
        return lax.ppermute(array.astype(jnp.bfloat16), axis, route)

    odd = place % 2 == 1
    packed = jnp.concatenate([first_mat, first_vec], axis=-1)
    pair_far = fill(swap(packed, 1), first_vec).astype(jnp.float32)
    joined = apply(jnp.where(odd, first_mat, pair_far[..., :width]), jnp.where(odd, pair_far, packed))
    total = joined.at[..., width:].add(jnp.where(odd, first_vec, pair_far[..., width:]))
    total = lax.dynamic_slice_in_dim(total, (place % 2) * half, half, 0)
    total_mat, total_vec = total[..., :width], total[..., width:]
    before_mat = before_vec = None
    bit = 2
    while bit < size:
        upper = (place // bit) % 2 == 1
        if 2 * bit >= size:
            route = [(i, i + bit) for i in range(size) if (i // bit) % 2 == 0]
            far_vec = lax.ppermute(total_vec.astype(jnp.bfloat16), axis, route)
            far_vec = fill(far_vec, total_vec).astype(jnp.float32)
            if before_mat is None:
                before_vec = far_vec
            else:
                before_vec = jnp.where(upper, apply(before_mat, far_vec) + before_vec, before_vec)
        else:
            packed = jnp.concatenate([total_mat, total_vec], axis=-1)
            far = fill(swap(packed, bit), total_vec).astype(jnp.float32)
            far_mat, far_vec = far[..., :width], far[..., width:]
            joined = apply(jnp.where(upper, total_mat, far_mat), jnp.where(upper, far, packed))
            new_mat = joined[..., :width]
            new_vec = joined[..., width:] + jnp.where(upper, total_vec, far_vec)
            if before_mat is None:
                identity = jnp.broadcast_to(jnp.eye(width, dtype=jnp.float32), total_mat.shape)
                before_mat = jnp.where(upper, far_mat, identity)
                before_vec = jnp.where(upper, far_vec, jnp.zeros_like(far_vec))
            else:
                joined = apply(before_mat, far)
                before_mat = jnp.where(upper, joined[..., :width], before_mat)
                before_vec = jnp.where(upper, joined[..., width:] + before_vec, before_vec)
            total_mat, total_vec = new_mat, new_vec
        bit *= 2
    other = fill(swap(before_vec, 1), before_vec).astype(jnp.float32)
    entering = jnp.where(
        odd,
        jnp.concatenate([other, before_vec], axis=0),
        jnp.concatenate([before_vec, other], axis=0),
    )
    entering = jnp.where(
        odd, apply(pair_far[..., :width], entering) + pair_far[..., width:], entering
    )
    while pending:
        work, inputs = pending.pop(0)
        done.append(work(*inputs))
    return entering, done


def passed_along(block, axis, distance):
    devices = range(lax.axis_size(axis))
    route = [(i - distance, i) for i in devices if i - distance in devices]
    return lax.ppermute(block, axis, route)


def unit_rows(array):
    return array / jnp.sqrt(jnp.sum(array * array, axis=-1, keepdims=True) + 1e-06)


def unit_inverse(lower_part):
    order_len = lower_part.shape[-1]
    identity = jnp.eye(order_len, dtype=jnp.float32)
    power = -lower_part
    total = identity + power
    steps = max(1, (order_len - 1).bit_length())
    if steps > 1:
        power = jnp.matmul(power, power, precision=highest)
    for counter in range(2, steps):
        both = jnp.matmul(
            jnp.stack([total, power]), jnp.stack([identity + power, power]), precision=highest
        )
        total, power = both[0], both[1]
    if steps > 1:
        total = jnp.matmul(total, identity + power, precision=highest)
    return total


def block_terms(keys_in, values_in, betas, log_rates):
    cumulative = jnp.cumsum(log_rates, axis=-1)
    length = keys_in.shape[-2]
    positions = jnp.arange(length)
    strict = positions[:, None] > positions[None, :]
    inclusive = positions[:, None] >= positions[None, :]
    spread = cumulative[..., :, None] - cumulative[..., None, :]
    ratio_strict = jnp.where(strict, jnp.exp(jnp.where(strict, spread, 0.0)), 0.0)
    key_gram = jnp.einsum("...td,...sd->...ts", keys_in, keys_in, precision=highest)
    inverse = unit_inverse(betas[..., :, None] * ratio_strict * key_gram)
    decayed = jnp.exp(cumulative)
    pseudo = jnp.matmul(inverse, betas[..., None] * values_in, precision=highest)
    writer = jnp.matmul(inverse, (betas * decayed)[..., None] * keys_in, precision=highest)
    to_end = jnp.exp(cumulative[..., -1:] - cumulative)
    keys_end = keys_in * to_end[..., None]
    identity = jnp.eye(keys_in.shape[-1], dtype=jnp.float32)
    transition = jnp.exp(cumulative[..., -1])[..., None, None] * identity - jnp.einsum(
        "...td,...te->...de", keys_end, writer, precision=highest
    )
    contrib = jnp.einsum("...td,...te->...de", keys_end, pseudo, precision=highest)
    return (transition, contrib, (keys_in, cumulative, decayed, pseudo, writer))


def block_outputs(queries, keys_in, cumulative, decayed, pseudo, writer):
    positions = jnp.arange(keys_in.shape[-2])
    inclusive = positions[:, None] >= positions[None, :]
    spread = cumulative[..., :, None] - cumulative[..., None, :]
    ratio_incl = jnp.where(inclusive, jnp.exp(jnp.where(inclusive, spread, 0.0)), 0.0)
    mixing = ratio_incl * jnp.einsum("...td,...sd->...ts", queries, keys_in, precision=highest)
    local_out = jnp.matmul(mixing, pseudo, precision=highest)
    carry_out = decayed[..., None] * queries - jnp.matmul(mixing, writer, precision=highest)
    return (local_out, carry_out)


def window_block(queries, keys_in, values_in, query_pos, key_pos):
    scores = jnp.einsum(
        "thd,shd->hts", queries, keys_in, preferred_element_type=jnp.float32
    ) * DH ** (-0.5)
    offsets = query_pos[:, None] - key_pos[None, :]
    inside = (offsets >= 0) & (offsets < WINDOW) & (key_pos[None, :] >= 0)
    masked = jnp.where(inside[None], scores, -1e30)
    block_max = jnp.max(masked, axis=-1)
    weights = jnp.where(inside[None], jnp.exp(masked - block_max[..., None]), 0.0)
    probs = weights.astype(jnp.bfloat16)
    block_num = jnp.einsum("hts,shd->htd", probs, values_in, preferred_element_type=jnp.float32)
    block_den = jnp.sum(weights, axis=-1)
    return (block_max, block_num, block_den)


def chain_pairs(earlier, later):
    matrix = jnp.einsum("hij,hjk->hik", later[0], earlier[0], precision=highest)
    vector = jnp.einsum("hij,hjk->hik", later[0], earlier[1], precision=highest) + later[1]
    return (matrix, vector)


def shards(
    delta_q,
    delta_k,
    delta_v,
    beta,
    log_decay,
    out_gate,
    norm_gain,
    attn_q,
    attn_k,
    attn_v,
    w_delta_out,
    w_attn_out,
):
    rows_here = delta_q.shape[0]
    local_heads = delta_q.shape[1] // DH
    block_len = min(64, rows_here)
    blocks = rows_here // block_len

    def heads_blocks(array):
        return (
            array.astype(jnp.float32)
            .reshape(blocks, block_len, local_heads, DH)
            .transpose(2, 0, 1, 3)
        )

    keys_in = unit_rows(heads_blocks(delta_k))
    values_in = heads_blocks(delta_v)
    betas = beta.reshape(blocks, block_len, local_heads).transpose(2, 0, 1)
    log_rates = log_decay.reshape(blocks, block_len, local_heads).transpose(2, 0, 1)
    transition, contrib, out_terms = block_terms(keys_in, values_in, betas, log_rates)
    identity = jnp.broadcast_to(jnp.eye(DH, dtype=jnp.float32), (local_heads, DH, DH))
    zero_state = jnp.zeros((local_heads, DH, DH), jnp.float32)
    start_mats = [identity]
    start_vecs = [zero_state]
    run_mat, run_vec = transition[:, 0], contrib[:, 0]
    for block in range(1, blocks):
        start_mats.append(run_mat)
        start_vecs.append(run_vec)
        joined = jnp.einsum(
            "hij,hjk->hik",
            transition[:, block],
            jnp.concatenate([run_mat, run_vec], axis=-1),
            precision=highest,
        )
        run_mat = joined[..., :DH]
        run_vec = joined[..., DH:] + contrib[:, block]
    shard_pair = (run_mat, run_vec)
    position = lax.axis_index("ctx")
    spans = WINDOW // rows_here
    far_blocks = [jnp.concatenate([attn_k, attn_v], axis=-1)]
    for back in range(1, spans + 1):
        far_blocks.append(passed_along(far_blocks[-1], "ctx", 1))
    far_blocks = far_blocks[1:]
    shard_pair, far_blocks = lax.optimization_barrier((shard_pair, far_blocks))

    def delta_local(delta_q, out_terms, start_mats, start_vecs):
        start_mats = jnp.stack(start_mats, axis=1)
        start_vecs = jnp.stack(start_vecs, axis=1)
        queries = unit_rows(heads_blocks(delta_q)) * DH ** (-0.5)
        local_out, carry_out = block_outputs(queries, *out_terms)
        own_out = local_out + jnp.einsum(
            "hntd,hnde->hnte", carry_out, start_vecs, precision=highest
        )
        reach = jnp.einsum("hntd,hnde->hnte", carry_out, start_mats, precision=highest)
        return own_out, reach

    key_width = attn_k.shape[1]

    def attend(query_rows, key_rows, value_rows, back):
        query_pos = position * rows_here + jnp.arange(rows_here, dtype=jnp.int32)
        key_pos = query_pos - back * rows_here
        return window_block(
            query_rows.reshape(rows_here, local_heads, DH),
            key_rows.reshape(rows_here, local_heads, DH),
            value_rows.reshape(rows_here, local_heads, DH),
            query_pos,
            key_pos,
        )

    def far_attend(query_rows, block, back):
        return attend(query_rows, block[:, :key_width], block[:, key_width:], back)

    def combine(w_attn_out, *parts):
        maxima = [part[0] for part in parts]
        top = maxima[0]
        for block_max in maxima[1:]:
            top = jnp.maximum(top, block_max)
        numer = jnp.zeros_like(parts[0][1])
        denom = jnp.zeros_like(parts[0][2])
        for block_max, block_num, block_den in parts:
            factor = jnp.exp(block_max - top)
            numer = numer + factor[..., None] * block_num
            denom = denom + factor * block_den
        attn_heads = (
            (numer / denom[..., None])
            .transpose(1, 0, 2)
            .reshape(rows_here, local_heads * DH)
            .astype(jnp.bfloat16)
        )
        return jnp.dot(attn_heads, w_attn_out, preferred_element_type=jnp.float32)

    fillers = [
        (delta_local, (delta_q, out_terms, start_mats, start_vecs)),
        (lambda q, k, v: attend(q, k, v, 0), (attn_q, attn_k, attn_v)),
    ]
    for back in range(1, spans + 1):
        fillers.append(
            (lambda q, blk, back=back: far_attend(q, blk, back), (attn_q, far_blocks[back - 1]))
        )
    incoming_state, results = prefix_state(shard_pair, "ctx", fillers)
    (own_out, reach), attn_parts = results[0], results[1:]
    attn_sum = combine(w_attn_out, *attn_parts)
    delta_raw = own_out + jnp.einsum("hntd,hde->hnte", reach, incoming_state, precision=highest)
    delta_raw = delta_raw.transpose(1, 2, 0, 3).reshape(rows_here, local_heads, DH)
    gate_act = jax.nn.silu(out_gate.astype(jnp.float32).reshape(rows_here, local_heads, DH))
    normed = (
        delta_raw
        / jnp.sqrt(jnp.mean(delta_raw * delta_raw, axis=-1, keepdims=True) + 1e-06)
        * norm_gain
        * gate_act
    )
    delta_heads = normed.reshape(rows_here, local_heads * DH).astype(jnp.bfloat16)
    running_partial_sum = attn_sum + jnp.dot(
        delta_heads, w_delta_out, preferred_element_type=jnp.float32
    )
    n_head = lax.axis_size("head")
    pieces = lax.all_to_all(
        running_partial_sum.astype(jnp.bfloat16), "head", 0, 0, tiled=True
    )
    pieces = pieces.reshape(n_head, rows_here // n_head, pieces.shape[-1]).astype(jnp.float32)
    return jnp.sum(pieces, axis=0).astype(jnp.bfloat16)


def solution(mesh):
    return jax.shard_map(
        shards,
        mesh=mesh,
        in_specs=(
            P("ctx", "head"),
            P("ctx", "head"),
            P("ctx", "head"),
            P("ctx", "head"),
            P("ctx", "head"),
            P("ctx", "head"),
            P(),
            P("ctx", "head"),
            P("ctx", "head"),
            P("ctx", "head"),
            P("head", None),
            P("head", None),
        ),
        out_specs=P(("ctx", "head"), None),
        check_vma=False,
    )
```

```python
import jax
import jax.numpy as jnp
from jax import lax
from jax.sharding import PartitionSpec as P

DH = 128
WINDOW = 1024


highest = lax.Precision.HIGHEST


def prefix_state(pair, axis, fillers):
    place = lax.axis_index(axis)
    size = lax.axis_size(axis)
    first_mat, first_vec = pair
    heads, width = first_mat.shape[0], first_mat.shape[-1]
    half = heads // 2
    done = []
    pending = list(fillers)

    def fill(far, gate):
        if not pending:
            return far
        work, inputs = pending.pop(0)
        inputs, _ = lax.optimization_barrier((inputs, gate))
        result, far = lax.optimization_barrier((work(*inputs), far))
        done.append(result)
        return far

    def apply(mat, far):
        return jnp.einsum("hij,hjk->hik", mat, far, precision=highest)

    def swap(array, bit):
        route = [(i, i ^ bit) for i in range(size)]
        return lax.ppermute(array.astype(jnp.bfloat16), axis, route)

    odd = place % 2 == 1
    packed = jnp.concatenate([first_mat, first_vec], axis=-1)
    pair_far = fill(swap(packed, 1), first_vec).astype(jnp.float32)
    joined = apply(jnp.where(odd, first_mat, pair_far[..., :width]), jnp.where(odd, pair_far, packed))
    total = joined.at[..., width:].add(jnp.where(odd, first_vec, pair_far[..., width:]))
    total = lax.dynamic_slice_in_dim(total, (place % 2) * half, half, 0)
    total_mat, total_vec = total[..., :width], total[..., width:]
    before_mat = before_vec = None
    bit = 2
    while bit < size:
        upper = (place // bit) % 2 == 1
        if 2 * bit >= size:
            route = [(i, i + bit) for i in range(size) if (i // bit) % 2 == 0]
            far_vec = lax.ppermute(total_vec.astype(jnp.bfloat16), axis, route)
            far_vec = fill(far_vec, total_vec).astype(jnp.float32)
            if before_mat is None:
                before_vec = far_vec
            else:
                before_vec = jnp.where(upper, apply(before_mat, far_vec) + before_vec, before_vec)
        else:
            packed = jnp.concatenate([total_mat, total_vec], axis=-1)
            far = fill(swap(packed, bit), total_vec).astype(jnp.float32)
            far_mat, far_vec = far[..., :width], far[..., width:]
            joined = apply(jnp.where(upper, total_mat, far_mat), jnp.where(upper, far, packed))
            new_mat = joined[..., :width]
            new_vec = joined[..., width:] + jnp.where(upper, total_vec, far_vec)
            if before_mat is None:
                identity = jnp.broadcast_to(jnp.eye(width, dtype=jnp.float32), total_mat.shape)
                before_mat = jnp.where(upper, far_mat, identity)
                before_vec = jnp.where(upper, far_vec, jnp.zeros_like(far_vec))
            else:
                joined = apply(before_mat, far)
                before_mat = jnp.where(upper, joined[..., :width], before_mat)
                before_vec = jnp.where(upper, joined[..., width:] + before_vec, before_vec)
            total_mat, total_vec = new_mat, new_vec
        bit *= 2
    other = fill(swap(before_vec, 1), before_vec).astype(jnp.float32)
    entering = jnp.where(
        odd,
        jnp.concatenate([other, before_vec], axis=0),
        jnp.concatenate([before_vec, other], axis=0),
    )
    entering = jnp.where(
        odd, apply(pair_far[..., :width], entering) + pair_far[..., width:], entering
    )
    while pending:
        work, inputs = pending.pop(0)
        done.append(work(*inputs))
    return entering, done


def fetch_back(block, axis, spans):
    size = lax.axis_size(axis)
    if spans != 4 or size % 2:
        return [passed_along(block, axis, back) for back in range(1, spans + 1)]
    even = lax.axis_index(axis) % 2 == 0

    def moved(array, pairs):
        return lax.ppermute(array, axis, [(i, j) for i, j in pairs if 0 <= j < size])

    evens = range(0, size, 2)
    one_back = passed_along(block, axis, 1)
    two_back = moved(block, [(i, i + 2) for i in evens])
    held = jnp.stack([one_back, two_back])
    from_even = moved(held, [(i, i + 2) for i in evens])
    from_pair = moved(held, [(i, i + 1) for i in evens])
    three_on = moved(one_back, [(i, i + 3) for i in evens])
    return [
        one_back,
        jnp.where(even, two_back, from_pair[0]),
        jnp.where(even, from_even[0], from_pair[1]),
        jnp.where(even, from_even[1], three_on),
    ]


def passed_along(block, axis, distance):
    devices = range(lax.axis_size(axis))
    route = [(i - distance, i) for i in devices if i - distance in devices]
    return lax.ppermute(block, axis, route)


def unit_rows(array):
    return array / jnp.sqrt(jnp.sum(array * array, axis=-1, keepdims=True) + 1e-06)


def unit_inverse(lower_part):
    order_len = lower_part.shape[-1]
    identity = jnp.eye(order_len, dtype=jnp.float32)
    power = -lower_part
    total = identity + power
    steps = max(1, (order_len - 1).bit_length())
    if steps > 1:
        power = jnp.matmul(power, power, precision=highest)
    for counter in range(2, steps):
        both = jnp.matmul(
            jnp.stack([total, power]), jnp.stack([identity + power, power]), precision=highest
        )
        total, power = both[0], both[1]
    if steps > 1:
        total = jnp.matmul(total, identity + power, precision=highest)
    return total


def block_terms(keys_in, values_in, betas, log_rates):
    cumulative = jnp.cumsum(log_rates, axis=-1)
    length = keys_in.shape[-2]
    positions = jnp.arange(length)
    strict = positions[:, None] > positions[None, :]
    inclusive = positions[:, None] >= positions[None, :]
    spread = cumulative[..., :, None] - cumulative[..., None, :]
    ratio_strict = jnp.where(strict, jnp.exp(jnp.where(strict, spread, 0.0)), 0.0)
    key_gram = jnp.einsum("...td,...sd->...ts", keys_in, keys_in, precision=highest)
    inverse = unit_inverse(betas[..., :, None] * ratio_strict * key_gram)
    decayed = jnp.exp(cumulative)
    pseudo = jnp.matmul(inverse, betas[..., None] * values_in, precision=highest)
    writer = jnp.matmul(inverse, (betas * decayed)[..., None] * keys_in, precision=highest)
    to_end = jnp.exp(cumulative[..., -1:] - cumulative)
    keys_end = keys_in * to_end[..., None]
    identity = jnp.eye(keys_in.shape[-1], dtype=jnp.float32)
    transition = jnp.exp(cumulative[..., -1])[..., None, None] * identity - jnp.einsum(
        "...td,...te->...de", keys_end, writer, precision=highest
    )
    contrib = jnp.einsum("...td,...te->...de", keys_end, pseudo, precision=highest)
    return (transition, contrib, (keys_in, cumulative, decayed, pseudo, writer))


def block_outputs(queries, keys_in, cumulative, decayed, pseudo, writer):
    positions = jnp.arange(keys_in.shape[-2])
    inclusive = positions[:, None] >= positions[None, :]
    spread = cumulative[..., :, None] - cumulative[..., None, :]
    ratio_incl = jnp.where(inclusive, jnp.exp(jnp.where(inclusive, spread, 0.0)), 0.0)
    mixing = ratio_incl * jnp.einsum("...td,...sd->...ts", queries, keys_in, precision=highest)
    local_out = jnp.matmul(mixing, pseudo, precision=highest)
    carry_out = decayed[..., None] * queries - jnp.matmul(mixing, writer, precision=highest)
    return (local_out, carry_out)


def window_block(queries, keys_in, values_in, query_pos, key_pos):
    scores = jnp.einsum(
        "thd,shd->hts", queries, keys_in, preferred_element_type=jnp.float32
    ) * DH ** (-0.5)
    offsets = query_pos[:, None] - key_pos[None, :]
    inside = (offsets >= 0) & (offsets < WINDOW) & (key_pos[None, :] >= 0)
    masked = jnp.where(inside[None], scores, -1e30)
    block_max = jnp.max(masked, axis=-1)
    weights = jnp.where(inside[None], jnp.exp(masked - block_max[..., None]), 0.0)
    probs = weights.astype(jnp.bfloat16)
    block_num = jnp.einsum("hts,shd->htd", probs, values_in, preferred_element_type=jnp.float32)
    block_den = jnp.sum(weights, axis=-1)
    return (block_max, block_num, block_den)


def chain_pairs(earlier, later):
    matrix = jnp.einsum("hij,hjk->hik", later[0], earlier[0], precision=highest)
    vector = jnp.einsum("hij,hjk->hik", later[0], earlier[1], precision=highest) + later[1]
    return (matrix, vector)


def shards(
    delta_q,
    delta_k,
    delta_v,
    beta,
    log_decay,
    out_gate,
    norm_gain,
    attn_q,
    attn_k,
    attn_v,
    w_delta_out,
    w_attn_out,
):
    rows_here = delta_q.shape[0]
    local_heads = delta_q.shape[1] // DH
    block_len = min(64, rows_here)
    blocks = rows_here // block_len

    def heads_blocks(array):
        return (
            array.astype(jnp.float32)
            .reshape(blocks, block_len, local_heads, DH)
            .transpose(2, 0, 1, 3)
        )

    keys_in = unit_rows(heads_blocks(delta_k))
    values_in = heads_blocks(delta_v)
    betas = beta.reshape(blocks, block_len, local_heads).transpose(2, 0, 1)
    log_rates = log_decay.reshape(blocks, block_len, local_heads).transpose(2, 0, 1)
    transition, contrib, out_terms = block_terms(keys_in, values_in, betas, log_rates)
    identity = jnp.broadcast_to(jnp.eye(DH, dtype=jnp.float32), (local_heads, DH, DH))
    zero_state = jnp.zeros((local_heads, DH, DH), jnp.float32)
    start_mats = [identity]
    start_vecs = [zero_state]
    run_mat, run_vec = transition[:, 0], contrib[:, 0]
    for block in range(1, blocks):
        start_mats.append(run_mat)
        start_vecs.append(run_vec)
        joined = jnp.einsum(
            "hij,hjk->hik",
            transition[:, block],
            jnp.concatenate([run_mat, run_vec], axis=-1),
            precision=highest,
        )
        run_mat = joined[..., :DH]
        run_vec = joined[..., DH:] + contrib[:, block]
    shard_pair = (run_mat, run_vec)
    position = lax.axis_index("ctx")
    spans = WINDOW // rows_here
    far_blocks = fetch_back(jnp.concatenate([attn_k, attn_v], axis=-1), "ctx", spans)
    shard_pair, far_blocks = lax.optimization_barrier((shard_pair, far_blocks))

    def delta_local(delta_q, out_terms, start_mats, start_vecs):
        start_mats = jnp.stack(start_mats, axis=1)
        start_vecs = jnp.stack(start_vecs, axis=1)
        queries = unit_rows(heads_blocks(delta_q)) * DH ** (-0.5)
        local_out, carry_out = block_outputs(queries, *out_terms)
        own_out = local_out + jnp.einsum(
            "hntd,hnde->hnte", carry_out, start_vecs, precision=highest
        )
        reach = jnp.einsum("hntd,hnde->hnte", carry_out, start_mats, precision=highest)
        return own_out, reach

    key_width = attn_k.shape[1]

    def attend(query_rows, key_rows, value_rows, back):
        query_pos = position * rows_here + jnp.arange(rows_here, dtype=jnp.int32)
        key_pos = query_pos - back * rows_here
        return window_block(
            query_rows.reshape(rows_here, local_heads, DH),
            key_rows.reshape(rows_here, local_heads, DH),
            value_rows.reshape(rows_here, local_heads, DH),
            query_pos,
            key_pos,
        )

    def far_attend(query_rows, block, back):
        return attend(query_rows, block[:, :key_width], block[:, key_width:], back)

    def combine(w_attn_out, *parts):
        maxima = [part[0] for part in parts]
        top = maxima[0]
        for block_max in maxima[1:]:
            top = jnp.maximum(top, block_max)
        numer = jnp.zeros_like(parts[0][1])
        denom = jnp.zeros_like(parts[0][2])
        for block_max, block_num, block_den in parts:
            factor = jnp.exp(block_max - top)
            numer = numer + factor[..., None] * block_num
            denom = denom + factor * block_den
        attn_heads = (
            (numer / denom[..., None])
            .transpose(1, 0, 2)
            .reshape(rows_here, local_heads * DH)
            .astype(jnp.bfloat16)
        )
        return jnp.dot(attn_heads, w_attn_out, preferred_element_type=jnp.float32)

    fillers = [
        (delta_local, (delta_q, out_terms, start_mats, start_vecs)),
        (lambda q, k, v: attend(q, k, v, 0), (attn_q, attn_k, attn_v)),
    ]
    for back in range(1, spans + 1):
        fillers.append(
            (lambda q, blk, back=back: far_attend(q, blk, back), (attn_q, far_blocks[back - 1]))
        )
    incoming_state, results = prefix_state(shard_pair, "ctx", fillers)
    (own_out, reach), attn_parts = results[0], results[1:]
    attn_sum = combine(w_attn_out, *attn_parts)
    delta_raw = own_out + jnp.einsum("hntd,hde->hnte", reach, incoming_state, precision=highest)
    delta_raw = delta_raw.transpose(1, 2, 0, 3).reshape(rows_here, local_heads, DH)
    gate_act = jax.nn.silu(out_gate.astype(jnp.float32).reshape(rows_here, local_heads, DH))
    normed = (
        delta_raw
        / jnp.sqrt(jnp.mean(delta_raw * delta_raw, axis=-1, keepdims=True) + 1e-06)
        * norm_gain
        * gate_act
    )
    delta_heads = normed.reshape(rows_here, local_heads * DH).astype(jnp.bfloat16)
    running_partial_sum = attn_sum + jnp.dot(
        delta_heads, w_delta_out, preferred_element_type=jnp.float32
    )
    n_head = lax.axis_size("head")
    pieces = lax.all_to_all(
        running_partial_sum.astype(jnp.bfloat16), "head", 0, 0, tiled=True
    )
    pieces = pieces.reshape(n_head, rows_here // n_head, pieces.shape[-1]).astype(jnp.float32)
    return jnp.sum(pieces, axis=0).astype(jnp.bfloat16)


def solution(mesh):
    return jax.shard_map(
        shards,
        mesh=mesh,
        in_specs=(
            P("ctx", "head"),
            P("ctx", "head"),
            P("ctx", "head"),
            P("ctx", "head"),
            P("ctx", "head"),
            P("ctx", "head"),
            P(),
            P("ctx", "head"),
            P("ctx", "head"),
            P("ctx", "head"),
            P("head", None),
            P("head", None),
        ),
        out_specs=P(("ctx", "head"), None),
        check_vma=False,
    )
```

```python
import jax
import jax.numpy as jnp
from jax import lax
from jax.sharding import PartitionSpec as P

DH = 128
WINDOW = 1024


highest = lax.Precision.HIGHEST


def prefix_state(pair, axis, fillers):
    place = lax.axis_index(axis)
    size = lax.axis_size(axis)
    first_mat, first_vec = pair
    heads, width = first_mat.shape[0], first_mat.shape[-1]
    half = heads // 2
    done = []
    pending = list(fillers)

    def fill(far, gate):
        if not pending:
            return far
        work, inputs = pending.pop(0)
        inputs, _ = lax.optimization_barrier((inputs, gate))
        result, far = lax.optimization_barrier((work(*inputs), far))
        done.append(result)
        return far

    def apply(mat, far):
        return jnp.einsum("hij,hjk->hik", mat, far, precision=highest)

    def swap(array, bit):
        route = [(i, i ^ bit) for i in range(size)]
        return lax.ppermute(array.astype(jnp.bfloat16), axis, route)

    odd = place % 2 == 1
    packed = jnp.concatenate([first_mat, first_vec], axis=-1)
    pair_far = fill(swap(packed, 1), first_vec).astype(jnp.float32)
    joined = apply(jnp.where(odd, first_mat, pair_far[..., :width]), jnp.where(odd, pair_far, packed))
    total = joined.at[..., width:].add(jnp.where(odd, first_vec, pair_far[..., width:]))
    total = lax.dynamic_slice_in_dim(total, (place % 2) * half, half, 0)
    total_mat, total_vec = total[..., :width], total[..., width:]
    before_mat = before_vec = None
    bit = 2
    while bit < size:
        upper = (place // bit) % 2 == 1
        if 2 * bit >= size:
            route = [(i, i + bit) for i in range(size) if (i // bit) % 2 == 0]
            far_vec = lax.ppermute(total_vec.astype(jnp.bfloat16), axis, route)
            far_vec = fill(far_vec, total_vec).astype(jnp.float32)
            if before_mat is None:
                before_vec = far_vec
            else:
                before_vec = jnp.where(upper, apply(before_mat, far_vec) + before_vec, before_vec)
        else:
            packed = jnp.concatenate([total_mat, total_vec], axis=-1)
            far = fill(swap(packed, bit), total_vec).astype(jnp.float32)
            far_mat, far_vec = far[..., :width], far[..., width:]
            joined = apply(jnp.where(upper, total_mat, far_mat), jnp.where(upper, far, packed))
            new_mat = joined[..., :width]
            new_vec = joined[..., width:] + jnp.where(upper, total_vec, far_vec)
            if before_mat is None:
                identity = jnp.broadcast_to(jnp.eye(width, dtype=jnp.float32), total_mat.shape)
                before_mat = jnp.where(upper, far_mat, identity)
                before_vec = jnp.where(upper, far_vec, jnp.zeros_like(far_vec))
            else:
                joined = apply(before_mat, far)
                before_mat = jnp.where(upper, joined[..., :width], before_mat)
                before_vec = jnp.where(upper, joined[..., width:] + before_vec, before_vec)
            total_mat, total_vec = new_mat, new_vec
        bit *= 2
    other = fill(swap(before_vec, 1), before_vec).astype(jnp.float32)
    entering = jnp.where(
        odd,
        jnp.concatenate([other, before_vec], axis=0),
        jnp.concatenate([before_vec, other], axis=0),
    )
    entering = jnp.where(
        odd, apply(pair_far[..., :width], entering) + pair_far[..., width:], entering
    )
    while pending:
        work, inputs = pending.pop(0)
        done.append(work(*inputs))
    return entering, done


def fetch_back(block, axis, spans):
    size = lax.axis_size(axis)
    if spans != 4 or size % 2:
        return [passed_along(block, axis, back) for back in range(1, spans + 1)]
    even = lax.axis_index(axis) % 2 == 0

    def moved(array, pairs):
        return lax.ppermute(array, axis, [(i, j) for i, j in pairs if 0 <= j < size])

    evens = range(0, size, 2)
    one_back = passed_along(block, axis, 1)
    two_back = moved(block, [(i, i + 2) for i in evens])
    held = jnp.stack([one_back, two_back])
    from_even = moved(held, [(i, i + 2) for i in evens])
    from_pair = moved(held, [(i, i + 1) for i in evens])
    three_on = moved(one_back, [(i, i + 3) for i in evens])
    return [
        one_back,
        jnp.where(even, two_back, from_pair[0]),
        jnp.where(even, from_even[0], from_pair[1]),
        jnp.where(even, from_even[1], three_on),
    ]


def passed_along(block, axis, distance):
    devices = range(lax.axis_size(axis))
    route = [(i - distance, i) for i in devices if i - distance in devices]
    return lax.ppermute(block, axis, route)


def unit_rows(array):
    return array / jnp.sqrt(jnp.sum(array * array, axis=-1, keepdims=True) + 1e-06)


def unit_inverse(lower_part):
    order_len = lower_part.shape[-1]
    identity = jnp.eye(order_len, dtype=jnp.float32)
    power = -lower_part
    total = identity + power
    steps = max(1, (order_len - 1).bit_length())
    if steps > 1:
        power = jnp.matmul(power, power, precision=highest)
    for counter in range(2, steps):
        both = jnp.matmul(
            jnp.stack([total, power]), jnp.stack([identity + power, power]), precision=highest
        )
        total, power = both[0], both[1]
    if steps > 1:
        total = jnp.matmul(total, identity + power, precision=highest)
    return total


def block_terms(keys_in, values_in, betas, log_rates):
    cumulative = jnp.cumsum(log_rates, axis=-1)
    length = keys_in.shape[-2]
    positions = jnp.arange(length)
    strict = positions[:, None] > positions[None, :]
    inclusive = positions[:, None] >= positions[None, :]
    spread = cumulative[..., :, None] - cumulative[..., None, :]
    ratio_strict = jnp.where(strict, jnp.exp(jnp.where(strict, spread, 0.0)), 0.0)
    key_gram = jnp.einsum("...td,...sd->...ts", keys_in, keys_in, precision=highest)
    inverse = unit_inverse(betas[..., :, None] * ratio_strict * key_gram)
    decayed = jnp.exp(cumulative)
    pseudo = jnp.matmul(inverse, betas[..., None] * values_in, precision=highest)
    writer = jnp.matmul(inverse, (betas * decayed)[..., None] * keys_in, precision=highest)
    to_end = jnp.exp(cumulative[..., -1:] - cumulative)
    keys_end = keys_in * to_end[..., None]
    identity = jnp.eye(keys_in.shape[-1], dtype=jnp.float32)
    transition = jnp.exp(cumulative[..., -1])[..., None, None] * identity - jnp.einsum(
        "...td,...te->...de", keys_end, writer, precision=highest
    )
    contrib = jnp.einsum("...td,...te->...de", keys_end, pseudo, precision=highest)
    return (transition, contrib, (keys_in, cumulative, decayed, pseudo, writer))


def block_outputs(queries, keys_in, cumulative, decayed, pseudo, writer):
    positions = jnp.arange(keys_in.shape[-2])
    inclusive = positions[:, None] >= positions[None, :]
    spread = cumulative[..., :, None] - cumulative[..., None, :]
    ratio_incl = jnp.where(inclusive, jnp.exp(jnp.where(inclusive, spread, 0.0)), 0.0)
    mixing = ratio_incl * jnp.einsum("...td,...sd->...ts", queries, keys_in, precision=highest)
    local_out = jnp.matmul(mixing, pseudo, precision=highest)
    carry_out = decayed[..., None] * queries - jnp.matmul(mixing, writer, precision=highest)
    return (local_out, carry_out)


def window_block(queries, keys_in, values_in, query_pos, key_pos):
    scores = jnp.einsum(
        "thd,shd->hts", queries, keys_in, preferred_element_type=jnp.float32
    ) * DH ** (-0.5)
    offsets = query_pos[:, None] - key_pos[None, :]
    inside = (offsets >= 0) & (offsets < WINDOW) & (key_pos[None, :] >= 0)
    masked = jnp.where(inside[None], scores, -1e30)
    block_max = jnp.max(masked, axis=-1)
    weights = jnp.where(inside[None], jnp.exp(masked - block_max[..., None]), 0.0)
    probs = weights.astype(jnp.bfloat16)
    block_num = jnp.einsum("hts,shd->htd", probs, values_in, preferred_element_type=jnp.float32)
    block_den = jnp.sum(weights, axis=-1)
    return (block_max, block_num, block_den)


def chain_pairs(earlier, later):
    matrix = jnp.einsum("hij,hjk->hik", later[0], earlier[0], precision=highest)
    vector = jnp.einsum("hij,hjk->hik", later[0], earlier[1], precision=highest) + later[1]
    return (matrix, vector)


def shards(
    delta_q,
    delta_k,
    delta_v,
    beta,
    log_decay,
    out_gate,
    norm_gain,
    attn_q,
    attn_k,
    attn_v,
    w_delta_out,
    w_attn_out,
):
    rows_here = delta_q.shape[0]
    local_heads = delta_q.shape[1] // DH
    block_len = min(64, rows_here)
    blocks = rows_here // block_len

    def heads_blocks(array):
        return (
            array.astype(jnp.float32)
            .reshape(blocks, block_len, local_heads, DH)
            .transpose(2, 0, 1, 3)
        )

    keys_in = unit_rows(heads_blocks(delta_k))
    values_in = heads_blocks(delta_v)
    betas = beta.reshape(blocks, block_len, local_heads).transpose(2, 0, 1)
    log_rates = log_decay.reshape(blocks, block_len, local_heads).transpose(2, 0, 1)
    transition, contrib, out_terms = block_terms(keys_in, values_in, betas, log_rates)
    identity = jnp.broadcast_to(jnp.eye(DH, dtype=jnp.float32), (local_heads, DH, DH))
    zero_state = jnp.zeros((local_heads, DH, DH), jnp.float32)
    start_mats = [identity]
    start_vecs = [zero_state]
    run_mat, run_vec = transition[:, 0], contrib[:, 0]
    for block in range(1, blocks):
        start_mats.append(run_mat)
        start_vecs.append(run_vec)
        joined = jnp.einsum(
            "hij,hjk->hik",
            transition[:, block],
            jnp.concatenate([run_mat, run_vec], axis=-1),
            precision=highest,
        )
        run_mat = joined[..., :DH]
        run_vec = joined[..., DH:] + contrib[:, block]
    shard_pair = (run_mat, run_vec)
    position = lax.axis_index("ctx")
    spans = WINDOW // rows_here
    far_blocks = fetch_back(jnp.concatenate([attn_k, attn_v], axis=-1), "ctx", spans)
    shard_pair, far_blocks = lax.optimization_barrier((shard_pair, far_blocks))

    def delta_local(delta_q, out_terms, start_mats, start_vecs):
        start_mats = jnp.stack(start_mats, axis=1)
        start_vecs = jnp.stack(start_vecs, axis=1)
        queries = unit_rows(heads_blocks(delta_q)) * DH ** (-0.5)
        local_out, carry_out = block_outputs(queries, *out_terms)
        own_out = local_out + jnp.einsum(
            "hntd,hnde->hnte", carry_out, start_vecs, precision=highest
        )
        reach = jnp.einsum("hntd,hnde->hnte", carry_out, start_mats, precision=highest)
        return own_out, reach

    key_width = attn_k.shape[1]

    def attend(query_rows, key_rows, value_rows, back):
        query_pos = position * rows_here + jnp.arange(rows_here, dtype=jnp.int32)
        key_pos = query_pos - back * rows_here
        return window_block(
            query_rows.reshape(rows_here, local_heads, DH),
            key_rows.reshape(rows_here, local_heads, DH),
            value_rows.reshape(rows_here, local_heads, DH),
            query_pos,
            key_pos,
        )

    def far_attend(query_rows, block, back):
        return attend(query_rows, block[:, :key_width], block[:, key_width:], back)

    def combine(w_attn_out, *parts):
        maxima = [part[0] for part in parts]
        top = maxima[0]
        for block_max in maxima[1:]:
            top = jnp.maximum(top, block_max)
        numer = jnp.zeros_like(parts[0][1])
        denom = jnp.zeros_like(parts[0][2])
        for block_max, block_num, block_den in parts:
            factor = jnp.exp(block_max - top)
            numer = numer + factor[..., None] * block_num
            denom = denom + factor * block_den
        attn_heads = (
            (numer / denom[..., None])
            .transpose(1, 0, 2)
            .reshape(rows_here, local_heads * DH)
            .astype(jnp.bfloat16)
        )
        return jnp.dot(attn_heads, w_attn_out, preferred_element_type=jnp.float32)

    fillers = [
        (delta_local, (delta_q, out_terms, start_mats, start_vecs)),
        (lambda q, k, v: attend(q, k, v, 0), (attn_q, attn_k, attn_v)),
    ]
    for back in range(1, spans + 1):
        fillers.append(
            (lambda q, blk, back=back: far_attend(q, blk, back), (attn_q, far_blocks[back - 1]))
        )
    incoming_state, results = prefix_state(shard_pair, "ctx", fillers)
    (own_out, reach), attn_parts = results[0], results[1:]
    attn_sum = combine(w_attn_out, *attn_parts)
    delta_raw = own_out + jnp.einsum("hntd,hde->hnte", reach, incoming_state, precision=highest)
    delta_raw = delta_raw.transpose(1, 2, 0, 3).reshape(rows_here, local_heads, DH)
    gate_act = jax.nn.silu(out_gate.astype(jnp.float32).reshape(rows_here, local_heads, DH))
    normed = (
        delta_raw
        / jnp.sqrt(jnp.mean(delta_raw * delta_raw, axis=-1, keepdims=True) + 1e-06)
        * norm_gain
        * gate_act
    )
    delta_heads = normed.reshape(rows_here, local_heads * DH).astype(jnp.bfloat16)
    running_partial_sum = attn_sum + jnp.dot(
        delta_heads, w_delta_out, preferred_element_type=jnp.float32
    )
    n_head = lax.axis_size("head")
    me = lax.axis_index("head")
    chunk = rows_here // n_head
    parts = running_partial_sum.astype(jnp.bfloat16)
    total = lax.dynamic_slice_in_dim(parts, me * chunk, chunk, 0).astype(jnp.float32)
    for shift in range(1, n_head):
        piece = lax.dynamic_slice_in_dim(parts, ((me + shift) % n_head) * chunk, chunk, 0)
        route = [(i, (i + shift) % n_head) for i in range(n_head)]
        total = total + lax.ppermute(piece, "head", route).astype(jnp.float32)
    return total.astype(jnp.bfloat16)


def solution(mesh):
    return jax.shard_map(
        shards,
        mesh=mesh,
        in_specs=(
            P("ctx", "head"),
            P("ctx", "head"),
            P("ctx", "head"),
            P("ctx", "head"),
            P("ctx", "head"),
            P("ctx", "head"),
            P(),
            P("ctx", "head"),
            P("ctx", "head"),
            P("ctx", "head"),
            P("head", None),
            P("head", None),
        ),
        out_specs=P(("ctx", "head"), None),
        check_vma=False,
    )
```

```python
import jax
import jax.numpy as jnp
from jax import lax
from jax.sharding import PartitionSpec as P

DH = 128
WINDOW = 1024


highest = lax.Precision.HIGHEST


def prefix_state(pair, axis, fillers):
    place = lax.axis_index(axis)
    size = lax.axis_size(axis)
    first_mat, first_vec = pair
    heads, width = first_mat.shape[0], first_mat.shape[-1]
    half = heads // 2
    done = []
    pending = list(fillers)

    def fill(far, gate):
        if not pending:
            return far
        work, inputs = pending.pop(0)
        inputs, _ = lax.optimization_barrier((inputs, gate))
        result, far = lax.optimization_barrier((work(*inputs), far))
        done.append(result)
        return far

    def apply(mat, far):
        return jnp.einsum("hij,hjk->hik", mat, far, precision=highest)

    def swap(array, bit):
        route = [(i, i ^ bit) for i in range(size)]
        return lax.ppermute(array.astype(jnp.bfloat16), axis, route)

    odd = place % 2 == 1
    packed = jnp.concatenate([first_mat, first_vec], axis=-1)
    pair_far = fill(swap(packed, 1), first_vec).astype(jnp.float32)
    joined = apply(jnp.where(odd, first_mat, pair_far[..., :width]), jnp.where(odd, pair_far, packed))
    total = joined.at[..., width:].add(jnp.where(odd, first_vec, pair_far[..., width:]))
    total = lax.dynamic_slice_in_dim(total, (place % 2) * half, half, 0)
    total_mat, total_vec = total[..., :width], total[..., width:]
    before_mat = before_vec = None
    bit = 2
    while bit < size:
        upper = (place // bit) % 2 == 1
        if 2 * bit >= size:
            route = [(i, i + bit) for i in range(size) if (i // bit) % 2 == 0]
            far_vec = lax.ppermute(total_vec.astype(jnp.bfloat16), axis, route)
            far_vec = fill(far_vec, total_vec).astype(jnp.float32)
            if before_mat is None:
                before_vec = far_vec
            else:
                before_vec = jnp.where(upper, apply(before_mat, far_vec) + before_vec, before_vec)
        else:
            packed = jnp.concatenate([total_mat, total_vec], axis=-1)
            far = fill(swap(packed, bit), total_vec).astype(jnp.float32)
            far_mat, far_vec = far[..., :width], far[..., width:]
            joined = apply(jnp.where(upper, total_mat, far_mat), jnp.where(upper, far, packed))
            new_mat = joined[..., :width]
            new_vec = joined[..., width:] + jnp.where(upper, total_vec, far_vec)
            if before_mat is None:
                identity = jnp.broadcast_to(jnp.eye(width, dtype=jnp.float32), total_mat.shape)
                before_mat = jnp.where(upper, far_mat, identity)
                before_vec = jnp.where(upper, far_vec, jnp.zeros_like(far_vec))
            else:
                joined = apply(before_mat, far)
                before_mat = jnp.where(upper, joined[..., :width], before_mat)
                before_vec = jnp.where(upper, joined[..., width:] + before_vec, before_vec)
            total_mat, total_vec = new_mat, new_vec
        bit *= 2
    other = fill(swap(before_vec, 1), before_vec).astype(jnp.float32)
    entering = jnp.where(
        odd,
        jnp.concatenate([other, before_vec], axis=0),
        jnp.concatenate([before_vec, other], axis=0),
    )
    entering = jnp.where(
        odd, apply(pair_far[..., :width], entering) + pair_far[..., width:], entering
    )
    while pending:
        work, inputs = pending.pop(0)
        done.append(work(*inputs))
    return entering, done


def fetch_back(block, axis, spans):
    size = lax.axis_size(axis)
    if spans != 4 or size % 2:
        return [passed_along(block, axis, back) for back in range(1, spans + 1)]
    even = lax.axis_index(axis) % 2 == 0

    def moved(array, pairs):
        return lax.ppermute(array, axis, [(i, j) for i, j in pairs if 0 <= j < size])

    evens = range(0, size, 2)
    one_back = passed_along(block, axis, 1)
    two_back = moved(block, [(i, i + 2) for i in evens])
    held = jnp.stack([one_back, two_back])
    from_even = moved(held, [(i, i + 2) for i in evens])
    from_pair = moved(held, [(i, i + 1) for i in evens])
    three_on = moved(from_even[0], [(i, i + 1) for i in evens])
    return [
        one_back,
        jnp.where(even, two_back, from_pair[0]),
        jnp.where(even, from_even[0], from_pair[1]),
        jnp.where(even, from_even[1], three_on),
    ]


def passed_along(block, axis, distance):
    devices = range(lax.axis_size(axis))
    route = [(i - distance, i) for i in devices if i - distance in devices]
    return lax.ppermute(block, axis, route)


def unit_rows(array):
    return array / jnp.sqrt(jnp.sum(array * array, axis=-1, keepdims=True) + 1e-06)


def unit_inverse(lower_part):
    order_len = lower_part.shape[-1]
    identity = jnp.eye(order_len, dtype=jnp.float32)
    power = -lower_part
    total = identity + power
    steps = max(1, (order_len - 1).bit_length())
    if steps > 1:
        power = jnp.matmul(power, power, precision=highest)
    for counter in range(2, steps):
        both = jnp.matmul(
            jnp.stack([total, power]), jnp.stack([identity + power, power]), precision=highest
        )
        total, power = both[0], both[1]
    if steps > 1:
        total = jnp.matmul(total, identity + power, precision=highest)
    return total


def block_terms(keys_in, values_in, betas, log_rates):
    cumulative = jnp.cumsum(log_rates, axis=-1)
    length = keys_in.shape[-2]
    positions = jnp.arange(length)
    strict = positions[:, None] > positions[None, :]
    inclusive = positions[:, None] >= positions[None, :]
    spread = cumulative[..., :, None] - cumulative[..., None, :]
    ratio_strict = jnp.where(strict, jnp.exp(jnp.where(strict, spread, 0.0)), 0.0)
    key_gram = jnp.einsum("...td,...sd->...ts", keys_in, keys_in, precision=highest)
    inverse = unit_inverse(betas[..., :, None] * ratio_strict * key_gram)
    decayed = jnp.exp(cumulative)
    pseudo = jnp.matmul(inverse, betas[..., None] * values_in, precision=highest)
    writer = jnp.matmul(inverse, (betas * decayed)[..., None] * keys_in, precision=highest)
    to_end = jnp.exp(cumulative[..., -1:] - cumulative)
    keys_end = keys_in * to_end[..., None]
    identity = jnp.eye(keys_in.shape[-1], dtype=jnp.float32)
    transition = jnp.exp(cumulative[..., -1])[..., None, None] * identity - jnp.einsum(
        "...td,...te->...de", keys_end, writer, precision=highest
    )
    contrib = jnp.einsum("...td,...te->...de", keys_end, pseudo, precision=highest)
    return (transition, contrib, (keys_in, cumulative, decayed, pseudo, writer))


def block_outputs(queries, keys_in, cumulative, decayed, pseudo, writer):
    positions = jnp.arange(keys_in.shape[-2])
    inclusive = positions[:, None] >= positions[None, :]
    spread = cumulative[..., :, None] - cumulative[..., None, :]
    ratio_incl = jnp.where(inclusive, jnp.exp(jnp.where(inclusive, spread, 0.0)), 0.0)
    mixing = ratio_incl * jnp.einsum("...td,...sd->...ts", queries, keys_in, precision=highest)
    local_out = jnp.matmul(mixing, pseudo, precision=highest)
    carry_out = decayed[..., None] * queries - jnp.matmul(mixing, writer, precision=highest)
    return (local_out, carry_out)


def window_block(queries, keys_in, values_in, query_pos, key_pos):
    scores = jnp.einsum(
        "thd,shd->hts", queries, keys_in, preferred_element_type=jnp.float32
    ) * DH ** (-0.5)
    offsets = query_pos[:, None] - key_pos[None, :]
    inside = (offsets >= 0) & (offsets < WINDOW) & (key_pos[None, :] >= 0)
    masked = jnp.where(inside[None], scores, -1e30)
    block_max = jnp.max(masked, axis=-1)
    weights = jnp.where(inside[None], jnp.exp(masked - block_max[..., None]), 0.0)
    probs = weights.astype(jnp.bfloat16)
    block_num = jnp.einsum("hts,shd->htd", probs, values_in, preferred_element_type=jnp.float32)
    block_den = jnp.sum(weights, axis=-1)
    return (block_max, block_num, block_den)


def chain_pairs(earlier, later):
    matrix = jnp.einsum("hij,hjk->hik", later[0], earlier[0], precision=highest)
    vector = jnp.einsum("hij,hjk->hik", later[0], earlier[1], precision=highest) + later[1]
    return (matrix, vector)


def shards(
    delta_q,
    delta_k,
    delta_v,
    beta,
    log_decay,
    out_gate,
    norm_gain,
    attn_q,
    attn_k,
    attn_v,
    w_delta_out,
    w_attn_out,
):
    rows_here = delta_q.shape[0]
    local_heads = delta_q.shape[1] // DH
    block_len = min(64, rows_here)
    blocks = rows_here // block_len

    def heads_blocks(array):
        return (
            array.astype(jnp.float32)
            .reshape(blocks, block_len, local_heads, DH)
            .transpose(2, 0, 1, 3)
        )

    keys_in = unit_rows(heads_blocks(delta_k))
    values_in = heads_blocks(delta_v)
    betas = beta.reshape(blocks, block_len, local_heads).transpose(2, 0, 1)
    log_rates = log_decay.reshape(blocks, block_len, local_heads).transpose(2, 0, 1)
    transition, contrib, out_terms = block_terms(keys_in, values_in, betas, log_rates)
    identity = jnp.broadcast_to(jnp.eye(DH, dtype=jnp.float32), (local_heads, DH, DH))
    zero_state = jnp.zeros((local_heads, DH, DH), jnp.float32)
    start_mats = [identity]
    start_vecs = [zero_state]
    run_mat, run_vec = transition[:, 0], contrib[:, 0]
    for block in range(1, blocks):
        start_mats.append(run_mat)
        start_vecs.append(run_vec)
        joined = jnp.einsum(
            "hij,hjk->hik",
            transition[:, block],
            jnp.concatenate([run_mat, run_vec], axis=-1),
            precision=highest,
        )
        run_mat = joined[..., :DH]
        run_vec = joined[..., DH:] + contrib[:, block]
    shard_pair = (run_mat, run_vec)
    position = lax.axis_index("ctx")
    spans = WINDOW // rows_here
    far_blocks = fetch_back(jnp.concatenate([attn_k, attn_v], axis=-1), "ctx", spans)
    shard_pair, far_blocks = lax.optimization_barrier((shard_pair, far_blocks))

    def delta_local(delta_q, out_terms, start_mats, start_vecs):
        start_mats = jnp.stack(start_mats, axis=1)
        start_vecs = jnp.stack(start_vecs, axis=1)
        queries = unit_rows(heads_blocks(delta_q)) * DH ** (-0.5)
        local_out, carry_out = block_outputs(queries, *out_terms)
        own_out = local_out + jnp.einsum(
            "hntd,hnde->hnte", carry_out, start_vecs, precision=highest
        )
        reach = jnp.einsum("hntd,hnde->hnte", carry_out, start_mats, precision=highest)
        return own_out, reach

    key_width = attn_k.shape[1]

    def attend(query_rows, key_rows, value_rows, back):
        query_pos = position * rows_here + jnp.arange(rows_here, dtype=jnp.int32)
        key_pos = query_pos - back * rows_here
        return window_block(
            query_rows.reshape(rows_here, local_heads, DH),
            key_rows.reshape(rows_here, local_heads, DH),
            value_rows.reshape(rows_here, local_heads, DH),
            query_pos,
            key_pos,
        )

    def far_attend(query_rows, block, back):
        return attend(query_rows, block[:, :key_width], block[:, key_width:], back)

    def combine(w_attn_out, *parts):
        maxima = [part[0] for part in parts]
        top = maxima[0]
        for block_max in maxima[1:]:
            top = jnp.maximum(top, block_max)
        numer = jnp.zeros_like(parts[0][1])
        denom = jnp.zeros_like(parts[0][2])
        for block_max, block_num, block_den in parts:
            factor = jnp.exp(block_max - top)
            numer = numer + factor[..., None] * block_num
            denom = denom + factor * block_den
        attn_heads = (
            (numer / denom[..., None])
            .transpose(1, 0, 2)
            .reshape(rows_here, local_heads * DH)
            .astype(jnp.bfloat16)
        )
        return jnp.dot(attn_heads, w_attn_out, preferred_element_type=jnp.float32)

    fillers = [
        (delta_local, (delta_q, out_terms, start_mats, start_vecs)),
        (lambda q, k, v: attend(q, k, v, 0), (attn_q, attn_k, attn_v)),
    ]
    for back in range(1, spans + 1):
        fillers.append(
            (lambda q, blk, back=back: far_attend(q, blk, back), (attn_q, far_blocks[back - 1]))
        )
    incoming_state, results = prefix_state(shard_pair, "ctx", fillers)
    (own_out, reach), attn_parts = results[0], results[1:]
    attn_sum = combine(w_attn_out, *attn_parts)
    delta_raw = own_out + jnp.einsum("hntd,hde->hnte", reach, incoming_state, precision=highest)
    delta_raw = delta_raw.transpose(1, 2, 0, 3).reshape(rows_here, local_heads, DH)
    gate_act = jax.nn.silu(out_gate.astype(jnp.float32).reshape(rows_here, local_heads, DH))
    normed = (
        delta_raw
        / jnp.sqrt(jnp.mean(delta_raw * delta_raw, axis=-1, keepdims=True) + 1e-06)
        * norm_gain
        * gate_act
    )
    delta_heads = normed.reshape(rows_here, local_heads * DH).astype(jnp.bfloat16)
    running_partial_sum = attn_sum + jnp.dot(
        delta_heads, w_delta_out, preferred_element_type=jnp.float32
    )
    n_head = lax.axis_size("head")
    pieces = lax.all_to_all(
        running_partial_sum.astype(jnp.bfloat16), "head", 0, 0, tiled=True
    )
    pieces = pieces.reshape(n_head, rows_here // n_head, pieces.shape[-1]).astype(jnp.float32)
    return jnp.sum(pieces, axis=0).astype(jnp.bfloat16)


def solution(mesh):
    return jax.shard_map(
        shards,
        mesh=mesh,
        in_specs=(
            P("ctx", "head"),
            P("ctx", "head"),
            P("ctx", "head"),
            P("ctx", "head"),
            P("ctx", "head"),
            P("ctx", "head"),
            P(),
            P("ctx", "head"),
            P("ctx", "head"),
            P("ctx", "head"),
            P("head", None),
            P("head", None),
        ),
        out_specs=P(("ctx", "head"), None),
        check_vma=False,
    )
```

```python
import jax
import jax.numpy as jnp
from jax import lax
from jax.sharding import PartitionSpec as P

DH = 128
WINDOW = 1024


highest = lax.Precision.HIGHEST


def prefix_state(pair, axis, fillers):
    place = lax.axis_index(axis)
    size = lax.axis_size(axis)
    first_mat, first_vec = pair
    heads, width = first_mat.shape[0], first_mat.shape[-1]
    half = heads // 2
    done = []
    pending = list(fillers)

    def fill(far, gate):
        if not pending:
            return far
        work, inputs = pending.pop(0)
        inputs, _ = lax.optimization_barrier((inputs, gate))
        result, far = lax.optimization_barrier((work(*inputs), far))
        done.append(result)
        return far

    def apply(mat, far):
        return jnp.einsum("hij,hjk->hik", mat, far, precision=highest)

    def swap(array, bit):
        route = [(i, i ^ bit) for i in range(size)]
        return lax.ppermute(array.astype(jnp.bfloat16), axis, route)

    odd = place % 2 == 1
    packed = jnp.concatenate([first_mat, first_vec], axis=-1)
    pair_far = fill(swap(packed, 1), first_vec).astype(jnp.float32)
    joined = apply(jnp.where(odd, first_mat, pair_far[..., :width]), jnp.where(odd, pair_far, packed))
    total = joined.at[..., width:].add(jnp.where(odd, first_vec, pair_far[..., width:]))
    total = lax.dynamic_slice_in_dim(total, (place % 2) * half, half, 0)
    total_mat, total_vec = total[..., :width], total[..., width:]
    before_mat = before_vec = None
    bit = 2
    while bit < size:
        upper = (place // bit) % 2 == 1
        if 2 * bit >= size:
            route = [(i, i + bit) for i in range(size) if (i // bit) % 2 == 0]
            far_vec = lax.ppermute(total_vec.astype(jnp.bfloat16), axis, route)
            far_vec = fill(far_vec, total_vec).astype(jnp.float32)
            if before_mat is None:
                before_vec = far_vec
            else:
                before_vec = jnp.where(upper, apply(before_mat, far_vec) + before_vec, before_vec)
        else:
            packed = jnp.concatenate([total_mat, total_vec], axis=-1)
            far = fill(swap(packed, bit), total_vec).astype(jnp.float32)
            far_mat, far_vec = far[..., :width], far[..., width:]
            joined = apply(jnp.where(upper, total_mat, far_mat), jnp.where(upper, far, packed))
            new_mat = joined[..., :width]
            new_vec = joined[..., width:] + jnp.where(upper, total_vec, far_vec)
            if before_mat is None:
                identity = jnp.broadcast_to(jnp.eye(width, dtype=jnp.float32), total_mat.shape)
                before_mat = jnp.where(upper, far_mat, identity)
                before_vec = jnp.where(upper, far_vec, jnp.zeros_like(far_vec))
            else:
                joined = apply(before_mat, far)
                before_mat = jnp.where(upper, joined[..., :width], before_mat)
                before_vec = jnp.where(upper, joined[..., width:] + before_vec, before_vec)
            total_mat, total_vec = new_mat, new_vec
        bit *= 2
    other = fill(swap(before_vec, 1), before_vec).astype(jnp.float32)
    entering = jnp.where(
        odd,
        jnp.concatenate([other, before_vec], axis=0),
        jnp.concatenate([before_vec, other], axis=0),
    )
    entering = jnp.where(
        odd, apply(pair_far[..., :width], entering) + pair_far[..., width:], entering
    )
    while pending:
        work, inputs = pending.pop(0)
        done.append(work(*inputs))
    return entering, done


def fetch_back(block, axis, spans):
    size = lax.axis_size(axis)
    if spans != 4 or size % 2:
        return [passed_along(block, axis, back) for back in range(1, spans + 1)]
    even = lax.axis_index(axis) % 2 == 0

    def moved(array, pairs):
        return lax.ppermute(array, axis, [(i, j) for i, j in pairs if 0 <= j < size])

    evens = range(0, size, 2)
    one_back = passed_along(block, axis, 1)
    two_back = moved(block, [(i, i + 2) for i in evens])
    held = jnp.stack([one_back, two_back])
    from_even = moved(held, [(i, i + 2) for i in evens])
    from_pair = moved(held, [(i, i + 1) for i in evens])
    three_on = moved(from_even[0], [(i, i + 1) for i in evens])
    return [
        one_back,
        jnp.where(even, two_back, from_pair[0]),
        jnp.where(even, from_even[0], from_pair[1]),
        jnp.where(even, from_even[1], three_on),
    ]


def passed_along(block, axis, distance):
    devices = range(lax.axis_size(axis))
    route = [(i - distance, i) for i in devices if i - distance in devices]
    return lax.ppermute(block, axis, route)


def unit_rows(array):
    return array / jnp.sqrt(jnp.sum(array * array, axis=-1, keepdims=True) + 1e-06)


def unit_inverse(lower_part):
    order_len = lower_part.shape[-1]
    identity = jnp.eye(order_len, dtype=jnp.float32)
    power = -lower_part
    total = identity + power
    steps = max(1, (order_len - 1).bit_length())
    if steps > 1:
        power = jnp.matmul(power, power, precision=highest)
    for counter in range(2, steps):
        both = jnp.matmul(
            jnp.stack([total, power]), jnp.stack([identity + power, power]), precision=highest
        )
        total, power = both[0], both[1]
    if steps > 1:
        total = jnp.matmul(total, identity + power, precision=highest)
    return total


def block_terms(keys_in, values_in, betas, log_rates):
    cumulative = jnp.cumsum(log_rates, axis=-1)
    length = keys_in.shape[-2]
    positions = jnp.arange(length)
    strict = positions[:, None] > positions[None, :]
    inclusive = positions[:, None] >= positions[None, :]
    spread = cumulative[..., :, None] - cumulative[..., None, :]
    ratio_strict = jnp.where(strict, jnp.exp(jnp.where(strict, spread, 0.0)), 0.0)
    key_gram = jnp.einsum("...td,...sd->...ts", keys_in, keys_in, precision=highest)
    inverse = unit_inverse(betas[..., :, None] * ratio_strict * key_gram)
    decayed = jnp.exp(cumulative)
    pseudo = jnp.matmul(inverse, betas[..., None] * values_in, precision=highest)
    writer = jnp.matmul(inverse, (betas * decayed)[..., None] * keys_in, precision=highest)
    to_end = jnp.exp(cumulative[..., -1:] - cumulative)
    keys_end = keys_in * to_end[..., None]
    identity = jnp.eye(keys_in.shape[-1], dtype=jnp.float32)
    transition = jnp.exp(cumulative[..., -1])[..., None, None] * identity - jnp.einsum(
        "...td,...te->...de", keys_end, writer, precision=highest
    )
    contrib = jnp.einsum("...td,...te->...de", keys_end, pseudo, precision=highest)
    return (transition, contrib, (keys_in, cumulative, decayed, pseudo, writer))


def block_outputs(queries, keys_in, cumulative, decayed, pseudo, writer):
    positions = jnp.arange(keys_in.shape[-2])
    inclusive = positions[:, None] >= positions[None, :]
    spread = cumulative[..., :, None] - cumulative[..., None, :]
    ratio_incl = jnp.where(inclusive, jnp.exp(jnp.where(inclusive, spread, 0.0)), 0.0)
    mixing = ratio_incl * jnp.einsum("...td,...sd->...ts", queries, keys_in, precision=highest)
    local_out = jnp.matmul(mixing, pseudo, precision=highest)
    carry_out = decayed[..., None] * queries - jnp.matmul(mixing, writer, precision=highest)
    return (local_out, carry_out)


def window_block(queries, keys_in, values_in, query_pos, key_pos):
    scores = jnp.einsum(
        "thd,shd->hts", queries, keys_in, preferred_element_type=jnp.float32
    ) * DH ** (-0.5)
    offsets = query_pos[:, None] - key_pos[None, :]
    inside = (offsets >= 0) & (offsets < WINDOW) & (key_pos[None, :] >= 0)
    masked = jnp.where(inside[None], scores, -1e30)
    block_max = jnp.max(masked, axis=-1)
    weights = jnp.where(inside[None], jnp.exp(masked - block_max[..., None]), 0.0)
    probs = weights.astype(jnp.bfloat16)
    block_num = jnp.einsum("hts,shd->htd", probs, values_in, preferred_element_type=jnp.float32)
    block_den = jnp.sum(weights, axis=-1)
    return (block_max, block_num, block_den)


def chain_pairs(earlier, later):
    matrix = jnp.einsum("hij,hjk->hik", later[0], earlier[0], precision=highest)
    vector = jnp.einsum("hij,hjk->hik", later[0], earlier[1], precision=highest) + later[1]
    return (matrix, vector)


def shards(
    delta_q,
    delta_k,
    delta_v,
    beta,
    log_decay,
    out_gate,
    norm_gain,
    attn_q,
    attn_k,
    attn_v,
    w_delta_out,
    w_attn_out,
):
    rows_here = delta_q.shape[0]
    local_heads = delta_q.shape[1] // DH
    block_len = min(64, rows_here)
    blocks = rows_here // block_len

    def heads_blocks(array):
        return (
            array.astype(jnp.float32)
            .reshape(blocks, block_len, local_heads, DH)
            .transpose(2, 0, 1, 3)
        )

    keys_in = unit_rows(heads_blocks(delta_k))
    values_in = heads_blocks(delta_v)
    betas = beta.reshape(blocks, block_len, local_heads).transpose(2, 0, 1)
    log_rates = log_decay.reshape(blocks, block_len, local_heads).transpose(2, 0, 1)
    transition, contrib, out_terms = block_terms(keys_in, values_in, betas, log_rates)
    identity = jnp.broadcast_to(jnp.eye(DH, dtype=jnp.float32), (local_heads, DH, DH))
    zero_state = jnp.zeros((local_heads, DH, DH), jnp.float32)
    start_mats = [identity]
    start_vecs = [zero_state]
    run_mat, run_vec = transition[:, 0], contrib[:, 0]
    for block in range(1, blocks):
        start_mats.append(run_mat)
        start_vecs.append(run_vec)
        joined = jnp.einsum(
            "hij,hjk->hik",
            transition[:, block],
            jnp.concatenate([run_mat, run_vec], axis=-1),
            precision=highest,
        )
        run_mat = joined[..., :DH]
        run_vec = joined[..., DH:] + contrib[:, block]
    shard_pair = (run_mat, run_vec)
    position = lax.axis_index("ctx")
    spans = WINDOW // rows_here
    far_blocks = fetch_back(jnp.concatenate([attn_k, attn_v], axis=-1), "ctx", spans)

    def delta_local(delta_q, out_terms, start_mats, start_vecs):
        start_mats = jnp.stack(start_mats, axis=1)
        start_vecs = jnp.stack(start_vecs, axis=1)
        queries = unit_rows(heads_blocks(delta_q)) * DH ** (-0.5)
        local_out, carry_out = block_outputs(queries, *out_terms)
        own_out = local_out + jnp.einsum(
            "hntd,hnde->hnte", carry_out, start_vecs, precision=highest
        )
        reach = jnp.einsum("hntd,hnde->hnte", carry_out, start_mats, precision=highest)
        return own_out, reach

    key_width = attn_k.shape[1]

    def attend(query_rows, key_rows, value_rows, back):
        query_pos = position * rows_here + jnp.arange(rows_here, dtype=jnp.int32)
        key_pos = query_pos - back * rows_here
        return window_block(
            query_rows.reshape(rows_here, local_heads, DH),
            key_rows.reshape(rows_here, local_heads, DH),
            value_rows.reshape(rows_here, local_heads, DH),
            query_pos,
            key_pos,
        )

    def far_attend(query_rows, block, back):
        return attend(query_rows, block[:, :key_width], block[:, key_width:], back)

    def combine(w_attn_out, *parts):
        maxima = [part[0] for part in parts]
        top = maxima[0]
        for block_max in maxima[1:]:
            top = jnp.maximum(top, block_max)
        numer = jnp.zeros_like(parts[0][1])
        denom = jnp.zeros_like(parts[0][2])
        for block_max, block_num, block_den in parts:
            factor = jnp.exp(block_max - top)
            numer = numer + factor[..., None] * block_num
            denom = denom + factor * block_den
        attn_heads = (
            (numer / denom[..., None])
            .transpose(1, 0, 2)
            .reshape(rows_here, local_heads * DH)
            .astype(jnp.bfloat16)
        )
        return jnp.dot(attn_heads, w_attn_out, preferred_element_type=jnp.float32)

    fillers = [
        (lambda *terms: (delta_local(*terms), far_blocks), (delta_q, out_terms, start_mats, start_vecs)),
        (lambda q, k, v: attend(q, k, v, 0), (attn_q, attn_k, attn_v)),
    ]
    for back in range(1, spans + 1):
        fillers.append(
            (lambda q, blk, back=back: far_attend(q, blk, back), (attn_q, far_blocks[back - 1]))
        )
    incoming_state, results = prefix_state(shard_pair, "ctx", fillers)
    ((own_out, reach), _), attn_parts = results[0], results[1:]
    attn_sum = combine(w_attn_out, *attn_parts)
    delta_raw = own_out + jnp.einsum("hntd,hde->hnte", reach, incoming_state, precision=highest)
    delta_raw = delta_raw.transpose(1, 2, 0, 3).reshape(rows_here, local_heads, DH)
    gate_act = jax.nn.silu(out_gate.astype(jnp.float32).reshape(rows_here, local_heads, DH))
    normed = (
        delta_raw
        / jnp.sqrt(jnp.mean(delta_raw * delta_raw, axis=-1, keepdims=True) + 1e-06)
        * norm_gain
        * gate_act
    )
    delta_heads = normed.reshape(rows_here, local_heads * DH).astype(jnp.bfloat16)
    running_partial_sum = attn_sum + jnp.dot(
        delta_heads, w_delta_out, preferred_element_type=jnp.float32
    )
    n_head = lax.axis_size("head")
    pieces = lax.all_to_all(
        running_partial_sum.astype(jnp.bfloat16), "head", 0, 0, tiled=True
    )
    pieces = pieces.reshape(n_head, rows_here // n_head, pieces.shape[-1]).astype(jnp.float32)
    return jnp.sum(pieces, axis=0).astype(jnp.bfloat16)


def solution(mesh):
    return jax.shard_map(
        shards,
        mesh=mesh,
        in_specs=(
            P("ctx", "head"),
            P("ctx", "head"),
            P("ctx", "head"),
            P("ctx", "head"),
            P("ctx", "head"),
            P("ctx", "head"),
            P(),
            P("ctx", "head"),
            P("ctx", "head"),
            P("ctx", "head"),
            P("head", None),
            P("head", None),
        ),
        out_specs=P(("ctx", "head"), None),
        check_vma=False,
    )
```

```python
import jax
import jax.numpy as jnp
from jax import lax
from jax.sharding import PartitionSpec as P

DH = 128
WINDOW = 1024


highest = lax.Precision.HIGHEST


def prefix_state(pair, axis, fillers):
    place = lax.axis_index(axis)
    size = lax.axis_size(axis)
    first_mat, first_vec = pair
    heads, width = first_mat.shape[0], first_mat.shape[-1]
    half = heads // 2
    done = []
    pending = list(fillers)

    def fill(far, gate):
        if not pending:
            return far
        work, inputs = pending.pop(0)
        inputs, _ = lax.optimization_barrier((inputs, gate))
        result, far = lax.optimization_barrier((work(*inputs), far))
        done.append(result)
        return far

    def apply(mat, far):
        return jnp.einsum("hij,hjk->hik", mat, far, precision=highest)

    def swap(array, bit):
        route = [(i, i ^ bit) for i in range(size)]
        return lax.ppermute(array.astype(jnp.bfloat16), axis, route)

    odd = place % 2 == 1
    packed = jnp.concatenate([first_mat, first_vec], axis=-1)
    pair_far = fill(swap(packed, 1), first_vec).astype(jnp.float32)
    joined = apply(jnp.where(odd, first_mat, pair_far[..., :width]), jnp.where(odd, pair_far, packed))
    total = joined.at[..., width:].add(jnp.where(odd, first_vec, pair_far[..., width:]))
    total = lax.dynamic_slice_in_dim(total, (place % 2) * half, half, 0)
    total_mat, total_vec = total[..., :width], total[..., width:]
    before_mat = before_vec = None
    bit = 2
    while bit < size:
        upper = (place // bit) % 2 == 1
        if 2 * bit >= size:
            route = [(i, i + bit) for i in range(size) if (i // bit) % 2 == 0]
            far_vec = lax.ppermute(total_vec.astype(jnp.bfloat16), axis, route)
            far_vec = fill(far_vec, total_vec).astype(jnp.float32)
            if before_mat is None:
                before_vec = far_vec
            else:
                before_vec = jnp.where(upper, apply(before_mat, far_vec) + before_vec, before_vec)
        else:
            packed = jnp.concatenate([total_mat, total_vec], axis=-1)
            far = fill(swap(packed, bit), total_vec).astype(jnp.float32)
            far_mat, far_vec = far[..., :width], far[..., width:]
            joined = apply(jnp.where(upper, total_mat, far_mat), jnp.where(upper, far, packed))
            new_mat = joined[..., :width]
            new_vec = joined[..., width:] + jnp.where(upper, total_vec, far_vec)
            if before_mat is None:
                identity = jnp.broadcast_to(jnp.eye(width, dtype=jnp.float32), total_mat.shape)
                before_mat = jnp.where(upper, far_mat, identity)
                before_vec = jnp.where(upper, far_vec, jnp.zeros_like(far_vec))
            else:
                joined = apply(before_mat, far)
                before_mat = jnp.where(upper, joined[..., :width], before_mat)
                before_vec = jnp.where(upper, joined[..., width:] + before_vec, before_vec)
            total_mat, total_vec = new_mat, new_vec
        bit *= 2
    other = fill(swap(before_vec, 1), before_vec).astype(jnp.float32)
    entering = jnp.where(
        odd,
        jnp.concatenate([other, before_vec], axis=0),
        jnp.concatenate([before_vec, other], axis=0),
    )
    entering = jnp.where(
        odd, apply(pair_far[..., :width], entering) + pair_far[..., width:], entering
    )
    while pending:
        work, inputs = pending.pop(0)
        done.append(work(*inputs))
    return entering, done


def fetch_back(block, axis, spans):
    size = lax.axis_size(axis)
    if spans != 4 or size % 2:
        return [passed_along(block, axis, back) for back in range(1, spans + 1)]
    even = lax.axis_index(axis) % 2 == 0

    def moved(array, pairs):
        return lax.ppermute(array, axis, [(i, j) for i, j in pairs if 0 <= j < size])

    evens = range(0, size, 2)
    one_back = passed_along(block, axis, 1)
    two_back = moved(block, [(i, i + 2) for i in evens])
    held = jnp.stack([one_back, two_back])
    from_even = moved(held, [(i, i + 2) for i in evens])
    from_pair = moved(held, [(i, i + 1) for i in evens])
    three_on = moved(from_even[0], [(i, i + 1) for i in evens])
    return [
        one_back,
        jnp.where(even, two_back, from_pair[0]),
        jnp.where(even, from_even[0], from_pair[1]),
        jnp.where(even, from_even[1], three_on),
    ]


def passed_along(block, axis, distance):
    devices = range(lax.axis_size(axis))
    route = [(i - distance, i) for i in devices if i - distance in devices]
    return lax.ppermute(block, axis, route)


def unit_rows(array):
    return array / jnp.sqrt(jnp.sum(array * array, axis=-1, keepdims=True) + 1e-06)


def unit_inverse(lower_part):
    order_len = lower_part.shape[-1]
    identity = jnp.eye(order_len, dtype=jnp.float32)
    power = -lower_part
    total = identity + power
    steps = max(1, (order_len - 1).bit_length())
    if steps > 1:
        power = jnp.matmul(power, power, precision=highest)
    for counter in range(2, steps):
        both = jnp.matmul(
            jnp.stack([total, power]), jnp.stack([identity + power, power]), precision=highest
        )
        total, power = both[0], both[1]
    if steps > 1:
        total = jnp.matmul(total, identity + power, precision=highest)
    return total


def block_terms(keys_in, values_in, betas, log_rates):
    cumulative = jnp.cumsum(log_rates, axis=-1)
    length = keys_in.shape[-2]
    positions = jnp.arange(length)
    strict = positions[:, None] > positions[None, :]
    inclusive = positions[:, None] >= positions[None, :]
    spread = cumulative[..., :, None] - cumulative[..., None, :]
    ratio_strict = jnp.where(strict, jnp.exp(jnp.where(strict, spread, 0.0)), 0.0)
    key_gram = jnp.einsum("...td,...sd->...ts", keys_in, keys_in, precision=highest)
    inverse = unit_inverse(betas[..., :, None] * ratio_strict * key_gram)
    decayed = jnp.exp(cumulative)
    pseudo = jnp.matmul(inverse, betas[..., None] * values_in, precision=highest)
    writer = jnp.matmul(inverse, (betas * decayed)[..., None] * keys_in, precision=highest)
    to_end = jnp.exp(cumulative[..., -1:] - cumulative)
    keys_end = keys_in * to_end[..., None]
    identity = jnp.eye(keys_in.shape[-1], dtype=jnp.float32)
    transition = jnp.exp(cumulative[..., -1])[..., None, None] * identity - jnp.einsum(
        "...td,...te->...de", keys_end, writer, precision=highest
    )
    contrib = jnp.einsum("...td,...te->...de", keys_end, pseudo, precision=highest)
    return (transition, contrib, (keys_in, cumulative, decayed, pseudo, writer))


def block_outputs(queries, keys_in, cumulative, decayed, pseudo, writer):
    positions = jnp.arange(keys_in.shape[-2])
    inclusive = positions[:, None] >= positions[None, :]
    spread = cumulative[..., :, None] - cumulative[..., None, :]
    ratio_incl = jnp.where(inclusive, jnp.exp(jnp.where(inclusive, spread, 0.0)), 0.0)
    mixing = ratio_incl * jnp.einsum("...td,...sd->...ts", queries, keys_in, precision=highest)
    local_out = jnp.matmul(mixing, pseudo, precision=highest)
    carry_out = decayed[..., None] * queries - jnp.matmul(mixing, writer, precision=highest)
    return (local_out, carry_out)


def window_block(queries, keys_in, values_in, query_pos, key_pos):
    scores = jnp.einsum(
        "thd,shd->hts", queries, keys_in, preferred_element_type=jnp.float32
    ) * DH ** (-0.5)
    offsets = query_pos[:, None] - key_pos[None, :]
    inside = (offsets >= 0) & (offsets < WINDOW) & (key_pos[None, :] >= 0)
    masked = jnp.where(inside[None], scores, -1e30)
    block_max = jnp.max(masked, axis=-1)
    weights = jnp.where(inside[None], jnp.exp(masked - block_max[..., None]), 0.0)
    probs = weights.astype(jnp.bfloat16)
    block_num = jnp.einsum("hts,shd->htd", probs, values_in, preferred_element_type=jnp.float32)
    block_den = jnp.sum(weights, axis=-1)
    return (block_max, block_num, block_den)


def chain_pairs(earlier, later):
    matrix = jnp.einsum("hij,hjk->hik", later[0], earlier[0], precision=highest)
    vector = jnp.einsum("hij,hjk->hik", later[0], earlier[1], precision=highest) + later[1]
    return (matrix, vector)


def shards(
    delta_q,
    delta_k,
    delta_v,
    beta,
    log_decay,
    out_gate,
    norm_gain,
    attn_q,
    attn_k,
    attn_v,
    w_delta_out,
    w_attn_out,
):
    rows_here = delta_q.shape[0]
    local_heads = delta_q.shape[1] // DH
    block_len = min(64, rows_here)
    blocks = rows_here // block_len

    def heads_blocks(array):
        return (
            array.astype(jnp.float32)
            .reshape(blocks, block_len, local_heads, DH)
            .transpose(2, 0, 1, 3)
        )

    keys_in = unit_rows(heads_blocks(delta_k))
    values_in = heads_blocks(delta_v)
    betas = beta.reshape(blocks, block_len, local_heads).transpose(2, 0, 1)
    log_rates = log_decay.reshape(blocks, block_len, local_heads).transpose(2, 0, 1)
    transition, contrib, out_terms = block_terms(keys_in, values_in, betas, log_rates)
    identity = jnp.broadcast_to(jnp.eye(DH, dtype=jnp.float32), (local_heads, DH, DH))
    zero_state = jnp.zeros((local_heads, DH, DH), jnp.float32)
    start_mats = [identity]
    start_vecs = [zero_state]
    run_mat, run_vec = transition[:, 0], contrib[:, 0]
    for block in range(1, blocks):
        start_mats.append(run_mat)
        start_vecs.append(run_vec)
        joined = jnp.einsum(
            "hij,hjk->hik",
            transition[:, block],
            jnp.concatenate([run_mat, run_vec], axis=-1),
            precision=highest,
        )
        run_mat = joined[..., :DH]
        run_vec = joined[..., DH:] + contrib[:, block]
    shard_pair = (run_mat, run_vec)
    position = lax.axis_index("ctx")
    spans = WINDOW // rows_here
    far_blocks = fetch_back(jnp.concatenate([attn_k, attn_v], axis=-1), "ctx", spans)

    def delta_local(delta_q, out_terms, start_mats, start_vecs):
        start_mats = jnp.stack(start_mats, axis=1)
        start_vecs = jnp.stack(start_vecs, axis=1)
        queries = unit_rows(heads_blocks(delta_q)) * DH ** (-0.5)
        local_out, carry_out = block_outputs(queries, *out_terms)
        own_out = local_out + jnp.einsum(
            "hntd,hnde->hnte", carry_out, start_vecs, precision=highest
        )
        reach = jnp.einsum("hntd,hnde->hnte", carry_out, start_mats, precision=highest)
        return own_out, reach

    key_width = attn_k.shape[1]

    def attend(query_rows, key_rows, value_rows, back):
        query_pos = position * rows_here + jnp.arange(rows_here, dtype=jnp.int32)
        key_pos = query_pos - back * rows_here
        return window_block(
            query_rows.reshape(rows_here, local_heads, DH),
            key_rows.reshape(rows_here, local_heads, DH),
            value_rows.reshape(rows_here, local_heads, DH),
            query_pos,
            key_pos,
        )

    def far_attend(query_rows, block, back):
        return attend(query_rows, block[:, :key_width], block[:, key_width:], back)

    def combine(w_attn_out, *parts):
        maxima = [part[0] for part in parts]
        top = maxima[0]
        for block_max in maxima[1:]:
            top = jnp.maximum(top, block_max)
        numer = jnp.zeros_like(parts[0][1])
        denom = jnp.zeros_like(parts[0][2])
        for block_max, block_num, block_den in parts:
            factor = jnp.exp(block_max - top)
            numer = numer + factor[..., None] * block_num
            denom = denom + factor * block_den
        attn_heads = (
            (numer / denom[..., None])
            .transpose(1, 0, 2)
            .reshape(rows_here, local_heads * DH)
            .astype(jnp.bfloat16)
        )
        return jnp.dot(attn_heads, w_attn_out, preferred_element_type=jnp.float32)

    fillers = [
        (
            lambda q, k, v: (attend(q, k, v, 0), far_blocks),
            (attn_q, attn_k, attn_v),
        ),
    ]
    for back in range(1, spans + 1):
        fillers.append(
            (lambda q, blk, back=back: far_attend(q, blk, back), (attn_q, far_blocks[back - 1]))
        )
    fillers.append((delta_local, (delta_q, out_terms, start_mats, start_vecs)))
    incoming_state, results = prefix_state(shard_pair, "ctx", fillers)
    own_out, reach = results[-1]
    attn_parts = [results[0][0]] + results[1:-1]
    attn_sum = combine(w_attn_out, *attn_parts)
    delta_raw = own_out + jnp.einsum("hntd,hde->hnte", reach, incoming_state, precision=highest)
    delta_raw = delta_raw.transpose(1, 2, 0, 3).reshape(rows_here, local_heads, DH)
    gate_act = jax.nn.silu(out_gate.astype(jnp.float32).reshape(rows_here, local_heads, DH))
    normed = (
        delta_raw
        / jnp.sqrt(jnp.mean(delta_raw * delta_raw, axis=-1, keepdims=True) + 1e-06)
        * norm_gain
        * gate_act
    )
    delta_heads = normed.reshape(rows_here, local_heads * DH).astype(jnp.bfloat16)
    running_partial_sum = attn_sum + jnp.dot(
        delta_heads, w_delta_out, preferred_element_type=jnp.float32
    )
    n_head = lax.axis_size("head")
    pieces = lax.all_to_all(
        running_partial_sum.astype(jnp.bfloat16), "head", 0, 0, tiled=True
    )
    pieces = pieces.reshape(n_head, rows_here // n_head, pieces.shape[-1]).astype(jnp.float32)
    return jnp.sum(pieces, axis=0).astype(jnp.bfloat16)


def solution(mesh):
    return jax.shard_map(
        shards,
        mesh=mesh,
        in_specs=(
            P("ctx", "head"),
            P("ctx", "head"),
            P("ctx", "head"),
            P("ctx", "head"),
            P("ctx", "head"),
            P("ctx", "head"),
            P(),
            P("ctx", "head"),
            P("ctx", "head"),
            P("ctx", "head"),
            P("head", None),
            P("head", None),
        ),
        out_specs=P(("ctx", "head"), None),
        check_vma=False,
    )
```

```python
import jax
import jax.numpy as jnp
from jax import lax
from jax.sharding import PartitionSpec as P

DH = 128
WINDOW = 1024


highest = lax.Precision.HIGHEST


def prefix_state(pair, axis, fillers):
    place = lax.axis_index(axis)
    size = lax.axis_size(axis)
    first_mat, first_vec = pair
    heads, width = first_mat.shape[0], first_mat.shape[-1]
    half = heads // 2
    done = []
    pending = list(fillers)

    def fill(far, gate):
        if not pending:
            return far
        work, inputs = pending.pop(0)
        inputs, _ = lax.optimization_barrier((inputs, gate))
        result, far = lax.optimization_barrier((work(*inputs), far))
        done.append(result)
        return far

    def apply(mat, far):
        return jnp.einsum("hij,hjk->hik", mat, far, precision=highest)

    def swap(array, bit):
        route = [(i, i ^ bit) for i in range(size)]
        return lax.ppermute(array.astype(jnp.bfloat16), axis, route)

    odd = place % 2 == 1
    packed = jnp.concatenate([first_mat, first_vec], axis=-1)
    pair_far = fill(swap(packed, 1), first_vec).astype(jnp.float32)
    joined = apply(jnp.where(odd, first_mat, pair_far[..., :width]), jnp.where(odd, pair_far, packed))
    total = joined.at[..., width:].add(jnp.where(odd, first_vec, pair_far[..., width:]))
    total = lax.dynamic_slice_in_dim(total, (place % 2) * half, half, 0)
    total_mat, total_vec = total[..., :width], total[..., width:]
    before_mat = before_vec = None
    bit = 2
    while bit < size:
        upper = (place // bit) % 2 == 1
        if 2 * bit >= size:
            route = [(i, i + bit) for i in range(size) if (i // bit) % 2 == 0]
            far_vec = lax.ppermute(total_vec.astype(jnp.bfloat16), axis, route)
            far_vec = fill(far_vec, total_vec).astype(jnp.float32)
            if before_mat is None:
                before_vec = far_vec
            else:
                before_vec = jnp.where(upper, apply(before_mat, far_vec) + before_vec, before_vec)
        else:
            packed = jnp.concatenate([total_mat, total_vec], axis=-1)
            far = fill(swap(packed, bit), total_vec).astype(jnp.float32)
            far_mat, far_vec = far[..., :width], far[..., width:]
            joined = apply(jnp.where(upper, total_mat, far_mat), jnp.where(upper, far, packed))
            new_mat = joined[..., :width]
            new_vec = joined[..., width:] + jnp.where(upper, total_vec, far_vec)
            if before_mat is None:
                identity = jnp.broadcast_to(jnp.eye(width, dtype=jnp.float32), total_mat.shape)
                before_mat = jnp.where(upper, far_mat, identity)
                before_vec = jnp.where(upper, far_vec, jnp.zeros_like(far_vec))
            else:
                joined = apply(before_mat, far)
                before_mat = jnp.where(upper, joined[..., :width], before_mat)
                before_vec = jnp.where(upper, joined[..., width:] + before_vec, before_vec)
            total_mat, total_vec = new_mat, new_vec
        bit *= 2
    other = fill(swap(before_vec, 1), before_vec).astype(jnp.float32)
    entering = jnp.where(
        odd,
        jnp.concatenate([other, before_vec], axis=0),
        jnp.concatenate([before_vec, other], axis=0),
    )
    entering = jnp.where(
        odd, apply(pair_far[..., :width], entering) + pair_far[..., width:], entering
    )
    while pending:
        work, inputs = pending.pop(0)
        done.append(work(*inputs))
    return entering, done


def fetch_back(block, axis, spans):
    size = lax.axis_size(axis)
    if spans != 4 or size % 2:
        return [passed_along(block, axis, back) for back in range(1, spans + 1)]
    even = lax.axis_index(axis) % 2 == 0

    def moved(array, pairs):
        return lax.ppermute(array, axis, [(i, j) for i, j in pairs if 0 <= j < size])

    evens = range(0, size, 2)
    one_back = passed_along(block, axis, 1)
    two_back = moved(block, [(i, i + 2) for i in evens])
    held = jnp.stack([one_back, two_back])
    from_even = moved(held, [(i, i + 2) for i in evens])
    from_pair = moved(held, [(i, i + 1) for i in evens])
    three_on = moved(from_even[0], [(i, i + 1) for i in evens])
    return [
        one_back,
        jnp.where(even, two_back, from_pair[0]),
        jnp.where(even, from_even[0], from_pair[1]),
        jnp.where(even, from_even[1], three_on),
    ]


def passed_along(block, axis, distance):
    devices = range(lax.axis_size(axis))
    route = [(i - distance, i) for i in devices if i - distance in devices]
    return lax.ppermute(block, axis, route)


def unit_rows(array):
    return array / jnp.sqrt(jnp.sum(array * array, axis=-1, keepdims=True) + 1e-06)


def unit_inverse(lower_part):
    order_len = lower_part.shape[-1]
    identity = jnp.eye(order_len, dtype=jnp.float32)
    power = -lower_part
    total = identity + power
    steps = max(1, (order_len - 1).bit_length())
    if steps > 1:
        power = jnp.matmul(power, power, precision=highest)
    for counter in range(2, steps):
        both = jnp.matmul(
            jnp.stack([total, power]), jnp.stack([identity + power, power]), precision=highest
        )
        total, power = both[0], both[1]
    if steps > 1:
        total = jnp.matmul(total, identity + power, precision=highest)
    return total


def block_terms(keys_in, values_in, betas, log_rates):
    cumulative = jnp.cumsum(log_rates, axis=-1)
    length = keys_in.shape[-2]
    positions = jnp.arange(length)
    strict = positions[:, None] > positions[None, :]
    inclusive = positions[:, None] >= positions[None, :]
    spread = cumulative[..., :, None] - cumulative[..., None, :]
    ratio_strict = jnp.where(strict, jnp.exp(jnp.where(strict, spread, 0.0)), 0.0)
    key_gram = jnp.einsum("...td,...sd->...ts", keys_in, keys_in, precision=highest)
    inverse = unit_inverse(betas[..., :, None] * ratio_strict * key_gram)
    decayed = jnp.exp(cumulative)
    pseudo = jnp.matmul(inverse, betas[..., None] * values_in, precision=highest)
    writer = jnp.matmul(inverse, (betas * decayed)[..., None] * keys_in, precision=highest)
    to_end = jnp.exp(cumulative[..., -1:] - cumulative)
    keys_end = keys_in * to_end[..., None]
    identity = jnp.eye(keys_in.shape[-1], dtype=jnp.float32)
    transition = jnp.exp(cumulative[..., -1])[..., None, None] * identity - jnp.einsum(
        "...td,...te->...de", keys_end, writer, precision=highest
    )
    contrib = jnp.einsum("...td,...te->...de", keys_end, pseudo, precision=highest)
    return (transition, contrib, (keys_in, cumulative, decayed, pseudo, writer))


def block_outputs(queries, keys_in, cumulative, decayed, pseudo, writer):
    positions = jnp.arange(keys_in.shape[-2])
    inclusive = positions[:, None] >= positions[None, :]
    spread = cumulative[..., :, None] - cumulative[..., None, :]
    ratio_incl = jnp.where(inclusive, jnp.exp(jnp.where(inclusive, spread, 0.0)), 0.0)
    mixing = ratio_incl * jnp.einsum("...td,...sd->...ts", queries, keys_in, precision=highest)
    local_out = jnp.matmul(mixing, pseudo, precision=highest)
    carry_out = decayed[..., None] * queries - jnp.matmul(mixing, writer, precision=highest)
    return (local_out, carry_out)


def window_block(queries, keys_in, values_in, query_pos, key_pos):
    scores = jnp.einsum(
        "thd,shd->hts", queries, keys_in, preferred_element_type=jnp.float32
    ) * DH ** (-0.5)
    offsets = query_pos[:, None] - key_pos[None, :]
    inside = (offsets >= 0) & (offsets < WINDOW) & (key_pos[None, :] >= 0)
    masked = jnp.where(inside[None], scores, -1e30)
    block_max = jnp.max(masked, axis=-1)
    weights = jnp.where(inside[None], jnp.exp(masked - block_max[..., None]), 0.0)
    probs = weights.astype(jnp.bfloat16)
    block_num = jnp.einsum("hts,shd->htd", probs, values_in, preferred_element_type=jnp.float32)
    block_den = jnp.sum(weights, axis=-1)
    return (block_max, block_num, block_den)


def chain_pairs(earlier, later):
    matrix = jnp.einsum("hij,hjk->hik", later[0], earlier[0], precision=highest)
    vector = jnp.einsum("hij,hjk->hik", later[0], earlier[1], precision=highest) + later[1]
    return (matrix, vector)


def shards(
    delta_q,
    delta_k,
    delta_v,
    beta,
    log_decay,
    out_gate,
    norm_gain,
    attn_q,
    attn_k,
    attn_v,
    w_delta_out,
    w_attn_out,
):
    rows_here = delta_q.shape[0]
    local_heads = delta_q.shape[1] // DH
    block_len = min(64, rows_here)
    blocks = rows_here // block_len

    def heads_blocks(array):
        return (
            array.astype(jnp.float32)
            .reshape(blocks, block_len, local_heads, DH)
            .transpose(2, 0, 1, 3)
        )

    keys_in = unit_rows(heads_blocks(delta_k))
    values_in = heads_blocks(delta_v)
    betas = beta.reshape(blocks, block_len, local_heads).transpose(2, 0, 1)
    log_rates = log_decay.reshape(blocks, block_len, local_heads).transpose(2, 0, 1)
    transition, contrib, out_terms = block_terms(keys_in, values_in, betas, log_rates)
    identity = jnp.broadcast_to(jnp.eye(DH, dtype=jnp.float32), (local_heads, DH, DH))
    zero_state = jnp.zeros((local_heads, DH, DH), jnp.float32)
    start_mats = [identity]
    start_vecs = [zero_state]
    run_mat, run_vec = transition[:, 0], contrib[:, 0]
    for block in range(1, blocks):
        start_mats.append(run_mat)
        start_vecs.append(run_vec)
        joined = jnp.einsum(
            "hij,hjk->hik",
            transition[:, block],
            jnp.concatenate([run_mat, run_vec], axis=-1),
            precision=highest,
        )
        run_mat = joined[..., :DH]
        run_vec = joined[..., DH:] + contrib[:, block]
    shard_pair = (run_mat, run_vec)
    position = lax.axis_index("ctx")
    spans = WINDOW // rows_here
    far_blocks = fetch_back(jnp.concatenate([attn_k, attn_v], axis=-1), "ctx", spans)

    def delta_local(delta_q, out_terms, start_mats, start_vecs):
        start_mats = jnp.stack(start_mats, axis=1)
        start_vecs = jnp.stack(start_vecs, axis=1)
        queries = unit_rows(heads_blocks(delta_q)) * DH ** (-0.5)
        local_out, carry_out = block_outputs(queries, *out_terms)
        own_out = local_out + jnp.einsum(
            "hntd,hnde->hnte", carry_out, start_vecs, precision=highest
        )
        reach = jnp.einsum("hntd,hnde->hnte", carry_out, start_mats, precision=highest)
        return own_out, reach

    key_width = attn_k.shape[1]

    def attend(query_rows, key_rows, value_rows, back):
        query_pos = position * rows_here + jnp.arange(rows_here, dtype=jnp.int32)
        key_pos = query_pos - back * rows_here
        return window_block(
            query_rows.reshape(rows_here, local_heads, DH),
            key_rows.reshape(rows_here, local_heads, DH),
            value_rows.reshape(rows_here, local_heads, DH),
            query_pos,
            key_pos,
        )

    def far_attend(query_rows, block, back):
        return attend(query_rows, block[:, :key_width], block[:, key_width:], back)

    def combine(w_attn_out, *parts):
        maxima = [part[0] for part in parts]
        top = maxima[0]
        for block_max in maxima[1:]:
            top = jnp.maximum(top, block_max)
        numer = jnp.zeros_like(parts[0][1])
        denom = jnp.zeros_like(parts[0][2])
        for block_max, block_num, block_den in parts:
            factor = jnp.exp(block_max - top)
            numer = numer + factor[..., None] * block_num
            denom = denom + factor * block_den
        attn_heads = (
            (numer / denom[..., None])
            .transpose(1, 0, 2)
            .reshape(rows_here, local_heads * DH)
            .astype(jnp.bfloat16)
        )
        return jnp.dot(attn_heads, w_attn_out, preferred_element_type=jnp.float32)

    fillers = [
        (delta_local, (delta_q, out_terms, start_mats, start_vecs)),
        (lambda q, k, v: (attend(q, k, v, 0), far_blocks), (attn_q, attn_k, attn_v)),
    ]
    for back in range(1, spans + 1):
        fillers.append(
            (lambda q, blk, back=back: far_attend(q, blk, back), (attn_q, far_blocks[back - 1]))
        )
    incoming_state, results = prefix_state(shard_pair, "ctx", fillers)
    own_out, reach = results[0]
    attn_parts = [results[1][0]] + results[2:]
    attn_sum = combine(w_attn_out, *attn_parts)
    delta_raw = own_out + jnp.einsum("hntd,hde->hnte", reach, incoming_state, precision=highest)
    delta_raw = delta_raw.transpose(1, 2, 0, 3).reshape(rows_here, local_heads, DH)
    gate_act = jax.nn.silu(out_gate.astype(jnp.float32).reshape(rows_here, local_heads, DH))
    normed = (
        delta_raw
        / jnp.sqrt(jnp.mean(delta_raw * delta_raw, axis=-1, keepdims=True) + 1e-06)
        * norm_gain
        * gate_act
    )
    delta_heads = normed.reshape(rows_here, local_heads * DH).astype(jnp.bfloat16)
    running_partial_sum = attn_sum + jnp.dot(
        delta_heads, w_delta_out, preferred_element_type=jnp.float32
    )
    n_head = lax.axis_size("head")
    pieces = lax.all_to_all(
        running_partial_sum.astype(jnp.bfloat16), "head", 0, 0, tiled=True
    )
    pieces = pieces.reshape(n_head, rows_here // n_head, pieces.shape[-1]).astype(jnp.float32)
    return jnp.sum(pieces, axis=0).astype(jnp.bfloat16)


def solution(mesh):
    return jax.shard_map(
        shards,
        mesh=mesh,
        in_specs=(
            P("ctx", "head"),
            P("ctx", "head"),
            P("ctx", "head"),
            P("ctx", "head"),
            P("ctx", "head"),
            P("ctx", "head"),
            P(),
            P("ctx", "head"),
            P("ctx", "head"),
            P("ctx", "head"),
            P("head", None),
            P("head", None),
        ),
        out_specs=P(("ctx", "head"), None),
        check_vma=False,
    )
```

```python
import jax
import jax.numpy as jnp
from jax import lax
from jax.sharding import PartitionSpec as P

DH = 128
WINDOW = 1024


highest = lax.Precision.HIGHEST


def prefix_state(pair, axis, fillers):
    place = lax.axis_index(axis)
    size = lax.axis_size(axis)
    first_mat, first_vec = pair
    heads, width = first_mat.shape[0], first_mat.shape[-1]
    half = heads // 2
    done = []
    pending = list(fillers)

    def fill(far, gate):
        if not pending:
            return far
        work, inputs = pending.pop(0)
        inputs, _ = lax.optimization_barrier((inputs, gate))
        result, far = lax.optimization_barrier((work(*inputs), far))
        done.append(result)
        return far

    def apply(mat, far):
        return jnp.einsum(
            "hij,hjk->hik",
            mat.astype(jnp.bfloat16),
            far.astype(jnp.bfloat16),
            preferred_element_type=jnp.float32,
        )

    def swap(array, bit):
        route = [(i, i ^ bit) for i in range(size)]
        return lax.ppermute(array.astype(jnp.bfloat16), axis, route)

    odd = place % 2 == 1
    packed = jnp.concatenate([first_mat, first_vec], axis=-1)
    pair_far = fill(swap(packed, 1), first_vec).astype(jnp.float32)
    joined = apply(jnp.where(odd, first_mat, pair_far[..., :width]), jnp.where(odd, pair_far, packed))
    total = joined.at[..., width:].add(jnp.where(odd, first_vec, pair_far[..., width:]))
    total = lax.dynamic_slice_in_dim(total, (place % 2) * half, half, 0)
    total_mat, total_vec = total[..., :width], total[..., width:]
    before_mat = before_vec = None
    bit = 2
    while bit < size:
        upper = (place // bit) % 2 == 1
        if 2 * bit >= size:
            route = [(i, i + bit) for i in range(size) if (i // bit) % 2 == 0]
            far_vec = lax.ppermute(total_vec.astype(jnp.bfloat16), axis, route)
            far_vec = fill(far_vec, total_vec).astype(jnp.float32)
            if before_mat is None:
                before_vec = far_vec
            else:
                before_vec = jnp.where(upper, apply(before_mat, far_vec) + before_vec, before_vec)
        else:
            packed = jnp.concatenate([total_mat, total_vec], axis=-1)
            far = fill(swap(packed, bit), total_vec).astype(jnp.float32)
            far_mat, far_vec = far[..., :width], far[..., width:]
            joined = apply(jnp.where(upper, total_mat, far_mat), jnp.where(upper, far, packed))
            new_mat = joined[..., :width]
            new_vec = joined[..., width:] + jnp.where(upper, total_vec, far_vec)
            if before_mat is None:
                identity = jnp.broadcast_to(jnp.eye(width, dtype=jnp.float32), total_mat.shape)
                before_mat = jnp.where(upper, far_mat, identity)
                before_vec = jnp.where(upper, far_vec, jnp.zeros_like(far_vec))
            else:
                joined = apply(before_mat, far)
                before_mat = jnp.where(upper, joined[..., :width], before_mat)
                before_vec = jnp.where(upper, joined[..., width:] + before_vec, before_vec)
            total_mat, total_vec = new_mat, new_vec
        bit *= 2
    other = fill(swap(before_vec, 1), before_vec).astype(jnp.float32)
    entering = jnp.where(
        odd,
        jnp.concatenate([other, before_vec], axis=0),
        jnp.concatenate([before_vec, other], axis=0),
    )
    entering = jnp.where(
        odd, apply(pair_far[..., :width], entering) + pair_far[..., width:], entering
    )
    while pending:
        work, inputs = pending.pop(0)
        done.append(work(*inputs))
    return entering, done


def fetch_back(block, axis, spans):
    size = lax.axis_size(axis)
    if spans != 4 or size % 2:
        return [passed_along(block, axis, back) for back in range(1, spans + 1)]
    even = lax.axis_index(axis) % 2 == 0

    def moved(array, pairs):
        return lax.ppermute(array, axis, [(i, j) for i, j in pairs if 0 <= j < size])

    evens = range(0, size, 2)
    one_back = passed_along(block, axis, 1)
    two_back = moved(block, [(i, i + 2) for i in evens])
    held = jnp.stack([one_back, two_back])
    from_even = moved(held, [(i, i + 2) for i in evens])
    from_pair = moved(held, [(i, i + 1) for i in evens])
    three_on = moved(from_even[0], [(i, i + 1) for i in evens])
    return [
        one_back,
        jnp.where(even, two_back, from_pair[0]),
        jnp.where(even, from_even[0], from_pair[1]),
        jnp.where(even, from_even[1], three_on),
    ]


def passed_along(block, axis, distance):
    devices = range(lax.axis_size(axis))
    route = [(i - distance, i) for i in devices if i - distance in devices]
    return lax.ppermute(block, axis, route)


def unit_rows(array):
    return array / jnp.sqrt(jnp.sum(array * array, axis=-1, keepdims=True) + 1e-06)


def unit_inverse(lower_part):
    order_len = lower_part.shape[-1]
    identity = jnp.eye(order_len, dtype=jnp.float32)
    power = -lower_part
    total = identity + power
    steps = max(1, (order_len - 1).bit_length())
    if steps > 1:
        power = jnp.matmul(power, power, precision=highest)
    for counter in range(2, steps):
        both = jnp.matmul(
            jnp.stack([total, power]), jnp.stack([identity + power, power]), precision=highest
        )
        total, power = both[0], both[1]
    if steps > 1:
        total = jnp.matmul(total, identity + power, precision=highest)
    return total


def block_terms(keys_in, values_in, betas, log_rates):
    cumulative = jnp.cumsum(log_rates, axis=-1)
    length = keys_in.shape[-2]
    positions = jnp.arange(length)
    strict = positions[:, None] > positions[None, :]
    inclusive = positions[:, None] >= positions[None, :]
    spread = cumulative[..., :, None] - cumulative[..., None, :]
    ratio_strict = jnp.where(strict, jnp.exp(jnp.where(strict, spread, 0.0)), 0.0)
    key_gram = jnp.einsum("...td,...sd->...ts", keys_in, keys_in, precision=highest)
    inverse = unit_inverse(betas[..., :, None] * ratio_strict * key_gram)
    decayed = jnp.exp(cumulative)
    pseudo = jnp.matmul(inverse, betas[..., None] * values_in, precision=highest)
    writer = jnp.matmul(inverse, (betas * decayed)[..., None] * keys_in, precision=highest)
    to_end = jnp.exp(cumulative[..., -1:] - cumulative)
    keys_end = keys_in * to_end[..., None]
    identity = jnp.eye(keys_in.shape[-1], dtype=jnp.float32)
    transition = jnp.exp(cumulative[..., -1])[..., None, None] * identity - jnp.einsum(
        "...td,...te->...de", keys_end, writer, precision=highest
    )
    contrib = jnp.einsum("...td,...te->...de", keys_end, pseudo, precision=highest)
    return (transition, contrib, (keys_in, cumulative, decayed, pseudo, writer))


def block_outputs(queries, keys_in, cumulative, decayed, pseudo, writer):
    positions = jnp.arange(keys_in.shape[-2])
    inclusive = positions[:, None] >= positions[None, :]
    spread = cumulative[..., :, None] - cumulative[..., None, :]
    ratio_incl = jnp.where(inclusive, jnp.exp(jnp.where(inclusive, spread, 0.0)), 0.0)
    mixing = ratio_incl * jnp.einsum("...td,...sd->...ts", queries, keys_in, precision=highest)
    local_out = jnp.matmul(mixing, pseudo, precision=highest)
    carry_out = decayed[..., None] * queries - jnp.matmul(mixing, writer, precision=highest)
    return (local_out, carry_out)


def window_block(queries, keys_in, values_in, query_pos, key_pos):
    scores = jnp.einsum(
        "thd,shd->hts", queries, keys_in, preferred_element_type=jnp.float32
    ) * DH ** (-0.5)
    offsets = query_pos[:, None] - key_pos[None, :]
    inside = (offsets >= 0) & (offsets < WINDOW) & (key_pos[None, :] >= 0)
    masked = jnp.where(inside[None], scores, -1e30)
    block_max = jnp.max(masked, axis=-1)
    weights = jnp.where(inside[None], jnp.exp(masked - block_max[..., None]), 0.0)
    probs = weights.astype(jnp.bfloat16)
    block_num = jnp.einsum("hts,shd->htd", probs, values_in, preferred_element_type=jnp.float32)
    block_den = jnp.sum(weights, axis=-1)
    return (block_max, block_num, block_den)


def chain_pairs(earlier, later):
    matrix = jnp.einsum("hij,hjk->hik", later[0], earlier[0], precision=highest)
    vector = jnp.einsum("hij,hjk->hik", later[0], earlier[1], precision=highest) + later[1]
    return (matrix, vector)


def shards(
    delta_q,
    delta_k,
    delta_v,
    beta,
    log_decay,
    out_gate,
    norm_gain,
    attn_q,
    attn_k,
    attn_v,
    w_delta_out,
    w_attn_out,
):
    rows_here = delta_q.shape[0]
    local_heads = delta_q.shape[1] // DH
    block_len = min(64, rows_here)
    blocks = rows_here // block_len

    def heads_blocks(array):
        return (
            array.astype(jnp.float32)
            .reshape(blocks, block_len, local_heads, DH)
            .transpose(2, 0, 1, 3)
        )

    keys_in = unit_rows(heads_blocks(delta_k))
    values_in = heads_blocks(delta_v)
    betas = beta.reshape(blocks, block_len, local_heads).transpose(2, 0, 1)
    log_rates = log_decay.reshape(blocks, block_len, local_heads).transpose(2, 0, 1)
    transition, contrib, out_terms = block_terms(keys_in, values_in, betas, log_rates)
    identity = jnp.broadcast_to(jnp.eye(DH, dtype=jnp.float32), (local_heads, DH, DH))
    zero_state = jnp.zeros((local_heads, DH, DH), jnp.float32)
    start_mats = [identity]
    start_vecs = [zero_state]
    run_mat, run_vec = transition[:, 0], contrib[:, 0]
    for block in range(1, blocks):
        start_mats.append(run_mat)
        start_vecs.append(run_vec)
        joined = jnp.einsum(
            "hij,hjk->hik",
            transition[:, block],
            jnp.concatenate([run_mat, run_vec], axis=-1),
            precision=highest,
        )
        run_mat = joined[..., :DH]
        run_vec = joined[..., DH:] + contrib[:, block]
    shard_pair = (run_mat, run_vec)
    position = lax.axis_index("ctx")
    spans = WINDOW // rows_here
    far_blocks = fetch_back(jnp.concatenate([attn_k, attn_v], axis=-1), "ctx", spans)

    def delta_local(delta_q, out_terms, start_mats, start_vecs):
        start_mats = jnp.stack(start_mats, axis=1)
        start_vecs = jnp.stack(start_vecs, axis=1)
        queries = unit_rows(heads_blocks(delta_q)) * DH ** (-0.5)
        local_out, carry_out = block_outputs(queries, *out_terms)
        own_out = local_out + jnp.einsum(
            "hntd,hnde->hnte", carry_out, start_vecs, precision=highest
        )
        reach = jnp.einsum("hntd,hnde->hnte", carry_out, start_mats, precision=highest)
        return own_out, reach

    key_width = attn_k.shape[1]

    def attend(query_rows, key_rows, value_rows, back):
        query_pos = position * rows_here + jnp.arange(rows_here, dtype=jnp.int32)
        key_pos = query_pos - back * rows_here
        return window_block(
            query_rows.reshape(rows_here, local_heads, DH),
            key_rows.reshape(rows_here, local_heads, DH),
            value_rows.reshape(rows_here, local_heads, DH),
            query_pos,
            key_pos,
        )

    def far_attend(query_rows, block, back):
        return attend(query_rows, block[:, :key_width], block[:, key_width:], back)

    def combine(w_attn_out, *parts):
        maxima = [part[0] for part in parts]
        top = maxima[0]
        for block_max in maxima[1:]:
            top = jnp.maximum(top, block_max)
        numer = jnp.zeros_like(parts[0][1])
        denom = jnp.zeros_like(parts[0][2])
        for block_max, block_num, block_den in parts:
            factor = jnp.exp(block_max - top)
            numer = numer + factor[..., None] * block_num
            denom = denom + factor * block_den
        attn_heads = (
            (numer / denom[..., None])
            .transpose(1, 0, 2)
            .reshape(rows_here, local_heads * DH)
            .astype(jnp.bfloat16)
        )
        return jnp.dot(attn_heads, w_attn_out, preferred_element_type=jnp.float32)

    fillers = [
        (delta_local, (delta_q, out_terms, start_mats, start_vecs)),
        (lambda q, k, v: (attend(q, k, v, 0), far_blocks), (attn_q, attn_k, attn_v)),
    ]
    for back in range(1, spans + 1):
        fillers.append(
            (lambda q, blk, back=back: far_attend(q, blk, back), (attn_q, far_blocks[back - 1]))
        )
    incoming_state, results = prefix_state(shard_pair, "ctx", fillers)
    own_out, reach = results[0]
    attn_parts = [results[1][0]] + results[2:]
    attn_sum = combine(w_attn_out, *attn_parts)
    delta_raw = own_out + jnp.einsum("hntd,hde->hnte", reach, incoming_state, precision=highest)
    delta_raw = delta_raw.transpose(1, 2, 0, 3).reshape(rows_here, local_heads, DH)
    gate_act = jax.nn.silu(out_gate.astype(jnp.float32).reshape(rows_here, local_heads, DH))
    normed = (
        delta_raw
        / jnp.sqrt(jnp.mean(delta_raw * delta_raw, axis=-1, keepdims=True) + 1e-06)
        * norm_gain
        * gate_act
    )
    delta_heads = normed.reshape(rows_here, local_heads * DH).astype(jnp.bfloat16)
    running_partial_sum = attn_sum + jnp.dot(
        delta_heads, w_delta_out, preferred_element_type=jnp.float32
    )
    n_head = lax.axis_size("head")
    pieces = lax.all_to_all(
        running_partial_sum.astype(jnp.bfloat16), "head", 0, 0, tiled=True
    )
    pieces = pieces.reshape(n_head, rows_here // n_head, pieces.shape[-1]).astype(jnp.float32)
    return jnp.sum(pieces, axis=0).astype(jnp.bfloat16)


def solution(mesh):
    return jax.shard_map(
        shards,
        mesh=mesh,
        in_specs=(
            P("ctx", "head"),
            P("ctx", "head"),
            P("ctx", "head"),
            P("ctx", "head"),
            P("ctx", "head"),
            P("ctx", "head"),
            P(),
            P("ctx", "head"),
            P("ctx", "head"),
            P("ctx", "head"),
            P("head", None),
            P("head", None),
        ),
        out_specs=P(("ctx", "head"), None),
        check_vma=False,
    )
```
